32 devices in a mesh: tok: 8 (over z, x), grp: 4 (over y, core).
Axes of the slice: x: 2, y: 2, z: 4, core: 2. Of those that a mesh axis runs over, the one named last changes fastest.
Arguments:
- queries: bfloat16 [1536, 2048], P('tok', 'grp'), may hold values from -72 to 72
- new_keys: bfloat16 [1536, 2048], P('tok', 'grp'), may hold values from -8 to 8
- new_values: bfloat16 [1536, 2048], P('tok', 'grp'), may hold values from -6 to 6
- residual: bfloat16 [1536, 2048], P('tok', 'grp'), may hold values from -6 to 6
- w_out: bfloat16 [2048, 2048], P('grp'), may hold values from -0.125 to 0.125
- leaf_keys: bfloat16 [8, 512, 2048], P('tok', None, 'grp'), may hold values from -6 to 6
- leaf_values: bfloat16 [8, 512, 2048], P('tok', None, 'grp'), may hold values from -6 to 6
- upper_keys: bfloat16 [6, 1024, 2048], P(None, 'tok', 'grp'), may hold values from -8 to 8
- upper_values: bfloat16 [6, 1024, 2048], P(None, 'tok', 'grp'), may hold values from -6 to 6
- req_len: int32 [8], replicated, may hold values from 48 to 192, as said below
- leaf_mid: int32 [8], replicated, may hold values from 0 to 3
- mid_root: int32 [4], replicated, may hold values from 0 to 1, as said below
- upper_len: int32 [6], replicated, may hold values from 256 to 1024, as said below
- leaf_len: int32 [8], replicated, may hold values from 128 to 512, as said below
Outputs:
- hidden_out: bfloat16 [1536, 2048], P('tok', 'grp')
The draws below stay inside these ranges and needn't reach their ends.
Inputs may be any that keep to these rules, and one draw needn't show every extreme that they name: `req_len`: some request has exactly 192 new tokens. `mid_root`: each root is the parent of 2 mids. `upper_len`: the first 2 entries are roots and equal 1024. `leaf_len`: some leaf has exactly 512 positions.
All inputs are finite; a program needn't handle non-finite values.
Results may differ from the reference program's by a relative error of at most 0.008.
Values may be sent and summed in bfloat16 or wider, within the bound.
No kernel may reach another device: no remote copies, remote signals or barrier semaphores. Data moves between devices by JAX's collectives and lax.ppermute only.
A program may use at most 64 MiB of HBM per device.

```python
import math
import jax
import jax.numpy as jnp
from jax import lax

D = 2048
HEADS = 16
HEAD_DIM = 128
HD = 2048
TOK_DEV = 192
LEAF_POS = 512
UPPER_LEN = 1024
ROOTS = 2
MIDS = 4
UPPERS = 6
REQS = 8
TOKENS = 1536


def draw_queries(key, part):
    sample = jnp.clip(3.0 * jax.random.normal(jax.random.fold_in(key, 7002), (TOKENS, HD), jnp.float32), -18.0, 18.0)
    return sample.astype(jnp.bfloat16)


def draw_new_keys(key, part):
    sample = jnp.clip(jax.random.normal(jax.random.fold_in(key, 7005), (TOKENS, HD), jnp.float32), -6.0, 6.0)
    return sample.astype(jnp.bfloat16)


def draw_upper_keys(key, part):
    sample = jnp.clip(jax.random.normal(jax.random.fold_in(key, 7030), (UPPERS, UPPER_LEN, HD), jnp.float32), -6.0, 6.0)
    return sample.astype(jnp.bfloat16)


def draw_req_len(key, part):
    drawn = jax.random.randint(jax.random.fold_in(key, 7020), (REQS,), TOK_DEV // 4, TOK_DEV + 1)
    chosen = jax.random.randint(jax.random.fold_in(key, 7021), (), 0, REQS)
    return jnp.where(jnp.arange(REQS) == chosen, TOK_DEV, drawn).astype(jnp.int32)


def draw_mid_root(key, part):
    return (jax.random.permutation(jax.random.fold_in(key, 7010), MIDS) % ROOTS).astype(jnp.int32)


def draw_upper_len(key, part):
    mids_len = jax.random.randint(jax.random.fold_in(key, 7011), (MIDS,), UPPER_LEN // 4, UPPER_LEN + 1)
    return jnp.concatenate([jnp.full((ROOTS,), UPPER_LEN, jnp.int32), mids_len.astype(jnp.int32)])


def draw_leaf_len(key, part):
    lengths_drawn = jax.random.randint(jax.random.fold_in(key, 7012), (REQS,), LEAF_POS // 4, LEAF_POS + 1)
    chosen = jax.random.randint(jax.random.fold_in(key, 7013), (), 0, REQS)
    return jnp.where(jnp.arange(REQS) == chosen, LEAF_POS, lengths_drawn).astype(jnp.int32)


def with_ends(values, rng, smallest, top_value):
    longest = values.shape.index(max(values.shape))
    spots = []
    for shift in (0, 1):
        where = [jax.random.randint(jax.random.fold_in(rng, axis), (), 0, length) for axis, length in enumerate(values.shape)]
        where[longest] = (where[longest] + shift) % values.shape[longest]
        spots.append(tuple(where))
    return values.at[spots[0]].set(smallest).at[spots[1]].set(top_value)


def block_scale(rng, extent, cuts, low, largest):
    loudness, own = 1.0, jax.random.fold_in(rng, 6)
    for position, shards_of in cuts:
        steps = jnp.exp(jax.random.uniform(jax.random.fold_in(own, position), (shards_of,), jnp.float32, low / len(cuts), largest / len(cuts)))
        loudness = loudness * jnp.repeat(steps, extent[position] // shards_of).reshape([-1 if axis == position else 1 for axis in range(len(extent))])
    return loudness


def bell_draw(own_key, extent, scale, most, cuts=(), kind=jnp.bfloat16):
    result = scale * jax.random.normal(own_key, extent, jnp.float32)
    if cuts:
        result = result * block_scale(own_key, extent, cuts, -0.22, 0.18)
    return jnp.clip(result, -most, most).astype(kind)


def setup_inputs(seed: int = 0) -> dict:
    key_list = jax.random.split(jax.random.key(seed), 15)
    return {
        "queries": draw_queries(jax.random.fold_in(key_list[14], 71), 0),
        "new_keys": draw_new_keys(jax.random.fold_in(key_list[14], 71), 0),
        "new_values": bell_draw(key_list[2], (TOKENS, HD), 1.0, 6.0, ((0, 8), (1, 4))),
        "residual": bell_draw(key_list[3], (TOKENS, D), 1.0, 6.0, ((0, 8), (1, 4))),
        "w_out": bell_draw(key_list[4], (HD, D), HD ** -0.5, 0.125, ((0, 4),)),
        "leaf_keys": bell_draw(key_list[5], (REQS, LEAF_POS, HD), 1.0, 6.0, ((0, 8), (2, 4))),
        "leaf_values": bell_draw(key_list[6], (REQS, LEAF_POS, HD), 1.0, 6.0, ((0, 8), (2, 4))),
        "upper_keys": draw_upper_keys(jax.random.fold_in(key_list[14], 71), 0),
        "upper_values": bell_draw(key_list[8], (UPPERS, UPPER_LEN, HD), 1.0, 6.0, ((1, 8), (2, 4))),
        "req_len": draw_req_len(jax.random.fold_in(key_list[14], 71), 0),
        "leaf_mid": with_ends(jax.random.randint(key_list[10], (REQS,), 0, MIDS), jax.random.fold_in(key_list[10], 1), 0, MIDS - 1).astype(jnp.int32),
        "mid_root": draw_mid_root(jax.random.fold_in(key_list[14], 71), 0),
        "upper_len": draw_upper_len(jax.random.fold_in(key_list[14], 71), 0),
        "leaf_len": draw_leaf_len(jax.random.fold_in(key_list[14], 71), 0),
    }


NEG_FILL = -1e+30

def heads_of(matrix):
    return matrix.astype(jnp.float32).reshape(matrix.shape[0], HEADS, HEAD_DIM)

def reference(queries, new_keys, new_values, residual, w_out, leaf_keys, leaf_values, upper_keys, upper_values, req_len, leaf_mid, mid_root, upper_len, leaf_len):
    score_scale = 1.0 / math.sqrt(HEAD_DIM)
    offsets = jnp.arange(TOK_DEV, dtype=jnp.int32)
    upper_pos = jnp.arange(UPPER_LEN, dtype=jnp.int32)
    leaf_pos = jnp.arange(LEAF_POS, dtype=jnp.int32)

    def one_request(request):
        is_valid = offsets < req_len[request]
        row_index = (request * TOK_DEV + offsets).astype(jnp.int32)
        mid_node = leaf_mid[request].astype(jnp.int32)
        root_node = mid_root[mid_node].astype(jnp.int32)
        mid_index = (ROOTS + mid_node).astype(jnp.int32)
        key_rows = jnp.concatenate([upper_keys[root_node], upper_keys[mid_index], leaf_keys[request], new_keys[row_index]], axis=0)
        value_rows = jnp.concatenate([upper_values[root_node], upper_values[mid_index], leaf_values[request], new_values[row_index]], axis=0)
        fixed_allowed = jnp.concatenate([upper_pos < upper_len[root_node], upper_pos < upper_len[mid_index], leaf_pos < leaf_len[request]])
        new_allowed = (offsets[None, :] <= offsets[:, None]) & is_valid[None, :]
        allowed = jnp.concatenate([jnp.broadcast_to(fixed_allowed[None, :], (TOK_DEV, fixed_allowed.shape[0])), new_allowed], axis=1)
        scores = jnp.einsum('qhd,khd->hqk', heads_of(queries[row_index]), heads_of(key_rows)) * score_scale
        scores = jnp.where(allowed[None], scores, NEG_FILL)
        row_max = lax.optimization_barrier(jnp.max(scores, axis=2, keepdims=True))
        exp_scores = jnp.where(allowed[None], jnp.exp(scores - row_max), 0.0)
        row_total = lax.optimization_barrier(jnp.sum(exp_scores, axis=2))
        weights = lax.optimization_barrier(exp_scores.astype(jnp.bfloat16)).astype(jnp.float32)
        weighted = jnp.einsum('hqk,khd->hqd', weights, heads_of(value_rows))
        attended = (weighted / row_total[:, :, None]).transpose(1, 0, 2).reshape(TOK_DEV, HEADS * HEAD_DIM)
        return jnp.where(is_valid[:, None], attended, 0.0).astype(jnp.bfloat16)
    attended = lax.map(one_request, jnp.arange(REQS, dtype=jnp.int32))
    attention = attended.reshape(TOKENS, HEADS * HEAD_DIM)
    projected = jnp.dot(attention, w_out, preferred_element_type=jnp.float32)
    return (residual.astype(jnp.float32) + projected).astype(jnp.bfloat16)
```

```python
import jax
import jax.numpy as jnp
from jax import lax
from jax.sharding import PartitionSpec as P

HEAD_DIM = 128


NEG_FILL = -1e30


def partial_attention(query_rows, key_rows, values, allowed, head_count):
    head_width = query_rows.shape[1] // head_count
    query_heads = query_rows.reshape(query_rows.shape[0], head_count, head_width)
    key_heads = key_rows.reshape(key_rows.shape[0], head_count, head_width)
    value_heads = values.reshape(values.shape[0], head_count, head_width)
    scores = jnp.einsum(
        "qhd,khd->hqk", query_heads, key_heads, preferred_element_type=jnp.float32
    ) * head_width ** (-0.5)
    scores = jnp.where(allowed[None], scores, NEG_FILL)
    row_max = jnp.max(scores, axis=2)
    exp_scores = jnp.where(allowed[None], jnp.exp(scores - row_max[:, :, None]), 0.0)
    row_total = jnp.sum(exp_scores, axis=2)
    weighted = jnp.einsum(
        "hqk,khd->hqd",
        exp_scores.astype(jnp.bfloat16),
        value_heads,
        preferred_element_type=jnp.float32,
    )
    return (row_max, row_total, weighted)


def combine(earlier, latter):
    new_max = jnp.maximum(earlier[0], latter[0])
    earlier_scale = jnp.exp(earlier[0] - new_max)
    latter_scale = jnp.exp(latter[0] - new_max)
    return (
        new_max,
        earlier[1] * earlier_scale + latter[1] * latter_scale,
        earlier[2] * earlier_scale[:, :, None] + latter[2] * latter_scale[:, :, None],
    )


def shards(
    queries,
    new_keys,
    new_values,
    residual,
    w_out,
    leaf_keys,
    leaf_values,
    upper_keys,
    upper_values,
    req_len,
    leaf_mid,
    mid_root,
    upper_len,
    leaf_len,
):
    dev_count = lax.axis_size("tok")
    my_index = lax.axis_index("tok")
    row_count = queries.shape[0]
    col_count = queries.shape[1]
    head_count = col_count // HEAD_DIM
    mid_count = mid_root.shape[0]
    node_count = upper_len.shape[0]
    root_count = node_count - mid_count
    chunk = upper_keys.shape[1]

    dest_mid = leaf_mid.astype(jnp.int32)
    dest_root = jnp.take(mid_root, dest_mid).astype(jnp.int32)
    dest_nodes = jnp.stack([dest_root, root_count + dest_mid], axis=1)
    send_keys = jnp.take(upper_keys, dest_nodes, axis=0)
    send_values = jnp.take(upper_values, dest_nodes, axis=0)
    recv_keys = lax.all_to_all(send_keys, "tok", 0, 0, tiled=True)
    recv_values = lax.all_to_all(send_values, "tok", 0, 0, tiled=True)

    owned = (jnp.arange(dev_count, dtype=jnp.int32) == my_index).astype(jnp.int32)
    my_length = jnp.sum(owned * req_len)
    my_mid = jnp.sum(owned * leaf_mid)
    my_leaf_len = jnp.sum(owned * leaf_len)
    my_root = jnp.sum((jnp.arange(mid_count) == my_mid).astype(jnp.int32) * mid_root)
    node_ids = jnp.arange(node_count)
    root_len = jnp.sum((node_ids == my_root).astype(jnp.int32) * upper_len)
    mid_len = jnp.sum((node_ids == root_count + my_mid).astype(jnp.int32) * upper_len)
    position = jnp.arange(row_count, dtype=jnp.int32)
    is_live = position < my_length
    leaf_count = leaf_keys.shape[1]
    local_keys = jnp.concatenate([leaf_keys[0], new_keys], axis=0)
    local_values = jnp.concatenate([leaf_values[0], new_values], axis=0)
    leaf_allowed = jnp.broadcast_to(
        (jnp.arange(leaf_count) < my_leaf_len)[None, :], (row_count, leaf_count)
    )
    new_allowed = (position[None, :] <= position[:, None]) & is_live[None, :]
    local_part = partial_attention(
        queries,
        local_keys,
        local_values,
        jnp.concatenate([leaf_allowed, new_allowed], axis=1),
        head_count,
    )

    upper_pos = (
        jnp.arange(dev_count, dtype=jnp.int32)[:, None, None] * chunk
        + jnp.arange(chunk, dtype=jnp.int32)[None, None, :]
    )
    upper_limit = jnp.stack([root_len, mid_len])[None, :, None]
    upper_ok = (upper_pos < upper_limit).reshape(-1)
    upper_part = partial_attention(
        queries,
        recv_keys.reshape(-1, col_count),
        recv_values.reshape(-1, col_count),
        jnp.broadcast_to(upper_ok[None, :], (row_count, upper_ok.shape[0])),
        head_count,
    )
    merged = combine(local_part, upper_part)
    attended = (merged[2] / merged[1][:, :, None]).transpose(1, 0, 2).reshape(row_count, col_count)
    attention = jnp.where(is_live[:, None], attended, 0.0).astype(jnp.bfloat16)
    projected = jnp.dot(attention, w_out, preferred_element_type=jnp.float32)
    mixed = lax.psum_scatter(
        projected.astype(jnp.bfloat16), "grp", scatter_dimension=1, tiled=True
    ).astype(jnp.float32)
    return (residual.astype(jnp.float32) + mixed).astype(jnp.bfloat16)


def solution(mesh):
    in_specs = (
        P("tok", "grp"),
        P("tok", "grp"),
        P("tok", "grp"),
        P("tok", "grp"),
        P("grp", None),
        P("tok", None, "grp"),
        P("tok", None, "grp"),
        P(None, "tok", "grp"),
        P(None, "tok", "grp"),
        P(),
        P(),
        P(),
        P(),
        P(),
    )
    out_specs = P("tok", "grp")
    return jax.shard_map(shards, mesh=mesh, in_specs=in_specs, out_specs=out_specs, check_vma=False)
```

```python
import jax
import jax.numpy as jnp
from jax import lax
from jax.sharding import PartitionSpec as P

HEAD_DIM = 128


NEG_FILL = -1e30


def partial_attention(query_rows, key_rows, values, allowed, head_count):
    head_width = query_rows.shape[1] // head_count
    parts = []
    for head in range(head_count):
        cols = slice(head * head_width, (head + 1) * head_width)
        scores = lax.dot_general(
            query_rows[:, cols],
            key_rows[:, cols],
            (((1,), (1,)), ((), ())),
            preferred_element_type=jnp.float32,
        ) * head_width ** (-0.5)
        scores = jnp.where(allowed, scores, NEG_FILL)
        row_max = jnp.max(scores, axis=1, keepdims=True)
        exp_scores = jnp.where(allowed, jnp.exp(scores - row_max), 0.0)
        row_total = jnp.sum(exp_scores, axis=1, keepdims=True)
        weighted = jnp.dot(
            exp_scores.astype(jnp.bfloat16),
            values[:, cols],
            preferred_element_type=jnp.float32,
        )
        parts.append((row_max, row_total, weighted))
    return parts


def combine(earlier, latter):
    merged = []
    for (max_a, total_a, sum_a), (max_b, total_b, sum_b) in zip(earlier, latter):
        new_max = jnp.maximum(max_a, max_b)
        scale_a = jnp.exp(max_a - new_max)
        scale_b = jnp.exp(max_b - new_max)
        merged.append(
            (new_max, total_a * scale_a + total_b * scale_b, sum_a * scale_a + sum_b * scale_b)
        )
    return merged


def shards(
    queries,
    new_keys,
    new_values,
    residual,
    w_out,
    leaf_keys,
    leaf_values,
    upper_keys,
    upper_values,
    req_len,
    leaf_mid,
    mid_root,
    upper_len,
    leaf_len,
):
    dev_count = lax.axis_size("tok")
    my_index = lax.axis_index("tok")
    row_count = queries.shape[0]
    col_count = queries.shape[1]
    head_count = col_count // HEAD_DIM
    mid_count = mid_root.shape[0]
    node_count = upper_len.shape[0]
    root_count = node_count - mid_count
    chunk = upper_keys.shape[1]

    dest_mid = leaf_mid.astype(jnp.int32)
    dest_root = jnp.take(mid_root, dest_mid).astype(jnp.int32)
    dest_nodes = jnp.stack([dest_root, root_count + dest_mid], axis=1)
    send = jnp.concatenate(
        [
            upper_keys.at[dest_nodes].get(mode="promise_in_bounds"),
            upper_values.at[dest_nodes].get(mode="promise_in_bounds"),
        ],
        axis=1,
    )
    received = lax.all_to_all(send, "tok", 0, 0, tiled=True)
    recv_keys = received[:, :2]
    recv_values = received[:, 2:]

    owned = (jnp.arange(dev_count, dtype=jnp.int32) == my_index).astype(jnp.int32)
    my_length = jnp.sum(owned * req_len)
    my_mid = jnp.sum(owned * leaf_mid)
    my_leaf_len = jnp.sum(owned * leaf_len)
    my_root = jnp.sum((jnp.arange(mid_count) == my_mid).astype(jnp.int32) * mid_root)
    node_ids = jnp.arange(node_count)
    root_len = jnp.sum((node_ids == my_root).astype(jnp.int32) * upper_len)
    mid_len = jnp.sum((node_ids == root_count + my_mid).astype(jnp.int32) * upper_len)
    position = jnp.arange(row_count, dtype=jnp.int32)
    is_live = position < my_length
    leaf_count = leaf_keys.shape[1]
    local_keys = jnp.concatenate([leaf_keys[0], new_keys], axis=0)
    local_values = jnp.concatenate([leaf_values[0], new_values], axis=0)
    leaf_allowed = jnp.broadcast_to(
        (jnp.arange(leaf_count) < my_leaf_len)[None, :], (row_count, leaf_count)
    )
    new_allowed = (position[None, :] <= position[:, None]) & is_live[None, :]
    local_part = partial_attention(
        queries,
        local_keys,
        local_values,
        jnp.concatenate([leaf_allowed, new_allowed], axis=1),
        head_count,
    )

    upper_pos = (
        jnp.arange(dev_count, dtype=jnp.int32)[:, None, None] * chunk
        + jnp.arange(chunk, dtype=jnp.int32)[None, None, :]
    )
    upper_limit = jnp.stack([root_len, mid_len])[None, :, None]
    upper_ok = (upper_pos < upper_limit).reshape(-1)
    upper_part = partial_attention(
        queries,
        recv_keys.reshape(-1, col_count),
        recv_values.reshape(-1, col_count),
        upper_ok[None, :],
        head_count,
    )
    merged = combine(local_part, upper_part)
    attended = jnp.concatenate([part[2] / part[1] for part in merged], axis=1)
    attention = jnp.where(is_live[:, None], attended, 0.0).astype(jnp.bfloat16)
    projected = jnp.dot(attention, w_out, preferred_element_type=jnp.float32)
    mixed = lax.psum_scatter(
        projected.astype(jnp.bfloat16), "grp", scatter_dimension=1, tiled=True
    ).astype(jnp.float32)
    return (residual.astype(jnp.float32) + mixed).astype(jnp.bfloat16)


def solution(mesh):
    in_specs = (
        P("tok", "grp"),
        P("tok", "grp"),
        P("tok", "grp"),
        P("tok", "grp"),
        P("grp", None),
        P("tok", None, "grp"),
        P("tok", None, "grp"),
        P(None, "tok", "grp"),
        P(None, "tok", "grp"),
        P(),
        P(),
        P(),
        P(),
        P(),
    )
    out_specs = P("tok", "grp")
    return jax.shard_map(shards, mesh=mesh, in_specs=in_specs, out_specs=out_specs, check_vma=False)
```

```python
import jax
import jax.numpy as jnp
from jax import lax
from jax.sharding import PartitionSpec as P

HEAD_DIM = 128


NEG_FILL = -1e30


def partial_attention(query_rows, key_rows, values, allowed, head_count):
    head_width = query_rows.shape[1] // head_count
    parts = []
    for head in range(head_count):
        cols = slice(head * head_width, (head + 1) * head_width)
        scores = lax.dot_general(
            query_rows[:, cols],
            key_rows[:, cols],
            (((1,), (1,)), ((), ())),
            preferred_element_type=jnp.float32,
        ) * head_width ** (-0.5)
        scores = jnp.where(allowed, scores, NEG_FILL)
        row_max = jnp.max(scores, axis=1, keepdims=True)
        exp_scores = jnp.where(allowed, jnp.exp(scores - row_max), 0.0)
        row_total = jnp.sum(exp_scores, axis=1, keepdims=True)
        weighted = jnp.dot(
            exp_scores.astype(jnp.bfloat16),
            values[:, cols],
            preferred_element_type=jnp.float32,
        )
        parts.append((row_max, row_total, weighted))
    return parts


def combine(earlier, latter):
    merged = []
    for (max_a, total_a, sum_a), (max_b, total_b, sum_b) in zip(earlier, latter):
        new_max = jnp.maximum(max_a, max_b)
        scale_a = jnp.exp(max_a - new_max)
        scale_b = jnp.exp(max_b - new_max)
        merged.append(
            (new_max, total_a * scale_a + total_b * scale_b, sum_a * scale_a + sum_b * scale_b)
        )
    return merged


def shards(
    queries,
    new_keys,
    new_values,
    residual,
    w_out,
    leaf_keys,
    leaf_values,
    upper_keys,
    upper_values,
    req_len,
    leaf_mid,
    mid_root,
    upper_len,
    leaf_len,
):
    dev_count = lax.axis_size("tok")
    my_index = lax.axis_index("tok")
    row_count = queries.shape[0]
    col_count = queries.shape[1]
    head_count = col_count // HEAD_DIM
    head_width = col_count // head_count
    mid_count = mid_root.shape[0]
    node_count = upper_len.shape[0]
    root_count = node_count - mid_count
    chunk = upper_keys.shape[1]

    owned = (jnp.arange(dev_count, dtype=jnp.int32) == my_index).astype(jnp.int32)
    my_length = jnp.sum(owned * req_len)
    my_mid = jnp.sum(owned * leaf_mid)
    my_leaf_len = jnp.sum(owned * leaf_len)
    my_root = jnp.sum((jnp.arange(mid_count) == my_mid).astype(jnp.int32) * mid_root)
    node_ids = jnp.arange(node_count)
    root_len = jnp.sum((node_ids == my_root).astype(jnp.int32) * upper_len)
    mid_len = jnp.sum((node_ids == root_count + my_mid).astype(jnp.int32) * upper_len)
    position = jnp.arange(row_count, dtype=jnp.int32)
    is_live = position < my_length
    leaf_count = leaf_keys.shape[1]
    local_keys = jnp.concatenate([leaf_keys[0], new_keys], axis=0)
    local_values = jnp.concatenate([leaf_values[0], new_values], axis=0)
    leaf_allowed = jnp.broadcast_to(
        (jnp.arange(leaf_count) < my_leaf_len)[None, :], (row_count, leaf_count)
    )
    new_allowed = (position[None, :] <= position[:, None]) & is_live[None, :]
    local_allowed = jnp.concatenate([leaf_allowed, new_allowed], axis=1)

    if dev_count * row_count * col_count * 4 <= (8 << 20):
        merged = query_plan(
            queries, local_keys, local_values, local_allowed, upper_keys, upper_values,
            leaf_mid, mid_root, upper_len, head_count, my_index, root_count, chunk,
        )
    else:
        merged = node_plan(
            queries, local_keys, local_values, local_allowed, upper_keys, upper_values,
            leaf_mid, mid_root, root_len, mid_len, head_count, root_count, chunk,
        )
    attended = jnp.concatenate([part[2] / part[1] for part in merged], axis=1)
    attention = jnp.where(is_live[:, None], attended, 0.0).astype(jnp.bfloat16)
    projected = jnp.dot(attention, w_out, preferred_element_type=jnp.float32)
    mixed = lax.psum_scatter(
        projected.astype(jnp.bfloat16), "grp", scatter_dimension=1, tiled=True
    ).astype(jnp.float32)
    return (residual.astype(jnp.float32) + mixed).astype(jnp.bfloat16)


def node_plan(
    queries, local_keys, local_values, local_allowed, upper_keys, upper_values,
    leaf_mid, mid_root, root_len, mid_len, head_count, root_count, chunk,
):
    dev_count = lax.axis_size("tok")
    col_count = queries.shape[1]
    dest_mid = leaf_mid.astype(jnp.int32)
    dest_root = jnp.take(mid_root, dest_mid).astype(jnp.int32)
    dest_nodes = jnp.stack([dest_root, root_count + dest_mid], axis=1)
    send = jnp.concatenate(
        [
            upper_keys.at[dest_nodes].get(mode="promise_in_bounds"),
            upper_values.at[dest_nodes].get(mode="promise_in_bounds"),
        ],
        axis=1,
    )
    received = lax.all_to_all(send, "tok", 0, 0, tiled=True)
    recv_keys = received[:, :2]
    recv_values = received[:, 2:]
    local_part = partial_attention(queries, local_keys, local_values, local_allowed, head_count)
    upper_pos = (
        jnp.arange(dev_count, dtype=jnp.int32)[:, None, None] * chunk
        + jnp.arange(chunk, dtype=jnp.int32)[None, None, :]
    )
    upper_limit = jnp.stack([root_len, mid_len])[None, :, None]
    upper_ok = (upper_pos < upper_limit).reshape(-1)
    upper_part = partial_attention(
        queries,
        recv_keys.reshape(-1, col_count),
        recv_values.reshape(-1, col_count),
        upper_ok[None, :],
        head_count,
    )
    return combine(local_part, upper_part)


def query_plan(
    queries, local_keys, local_values, local_allowed, upper_keys, upper_values,
    leaf_mid, mid_root, upper_len, head_count, my_index, root_count, chunk,
):
    dev_count = lax.axis_size("tok")
    row_count = queries.shape[0]
    col_count = queries.shape[1]
    head_width = col_count // head_count
    node_count = upper_keys.shape[0]
    scale = head_width ** (-0.5)
    all_queries = lax.all_gather(queries, "tok", axis=0, tiled=True)
    req_mid = leaf_mid.astype(jnp.int32)
    req_root = jnp.take(mid_root, req_mid).astype(jnp.int32)
    node_ids = jnp.arange(node_count, dtype=jnp.int32)
    node_used = (node_ids[None, :] == req_root[:, None]) | (
        node_ids[None, :] == root_count + req_mid[:, None]
    )
    pos_ok = (my_index * chunk + jnp.arange(chunk, dtype=jnp.int32))[None, :] < upper_len[:, None]
    seen = (node_used[:, :, None] & pos_ok[None, :, :]).reshape(dev_count, 1, node_count * chunk)
    flat_keys = upper_keys.reshape(node_count * chunk, col_count)
    flat_values = upper_values.reshape(node_count * chunk, col_count)

    upper_scores = []
    local_scores = []
    maxima = []
    for head in range(head_count):
        cols = slice(head * head_width, (head + 1) * head_width)
        scores = lax.dot_general(
            all_queries[:, cols], flat_keys[:, cols], (((1,), (1,)), ((), ())),
            preferred_element_type=jnp.float32,
        ) * scale
        scores = jnp.where(seen, scores.reshape(dev_count, row_count, -1), NEG_FILL)
        upper_max = jnp.max(scores, axis=2)
        own = lax.dynamic_slice_in_dim(upper_max, my_index, 1, axis=0)
        mine = lax.dot_general(
            queries[:, cols], local_keys[:, cols], (((1,), (1,)), ((), ())),
            preferred_element_type=jnp.float32,
        ) * scale
        mine = jnp.where(local_allowed, mine, NEG_FILL)
        own = jnp.maximum(own, jnp.max(mine, axis=1)[None, :])
        maxima.append(lax.dynamic_update_slice_in_dim(upper_max, own, my_index, axis=0))
        upper_scores.append(scores)
        local_scores.append(mine)
    row_max = lax.pmax(jnp.stack(maxima, axis=2), "tok")
    sums = []
    totals = []
    for head in range(head_count):
        cols = slice(head * head_width, (head + 1) * head_width)
        head_max = row_max[:, :, head : head + 1]
        exps = jnp.where(seen, jnp.exp(upper_scores[head] - head_max), 0.0)
        totals.append(jnp.sum(exps, axis=2))
        sums.append(
            jnp.dot(
                exps.reshape(dev_count * row_count, -1).astype(jnp.bfloat16),
                flat_values[:, cols],
                preferred_element_type=jnp.float32,
            )
        )
    upper_sum, upper_total = lax.psum_scatter(
        (jnp.concatenate(sums, axis=1), jnp.stack(totals, axis=2).reshape(dev_count * row_count, head_count)),
        "tok",
        scatter_dimension=0,
        tiled=True,
    )
    own_max = lax.dynamic_index_in_dim(row_max, my_index, axis=0, keepdims=False)
    merged = []
    for head in range(head_count):
        cols = slice(head * head_width, (head + 1) * head_width)
        exps = jnp.where(
            local_allowed, jnp.exp(local_scores[head] - own_max[:, head : head + 1]), 0.0
        )
        total = jnp.sum(exps, axis=1, keepdims=True) + upper_total[:, head : head + 1]
        weighted = jnp.dot(
            exps.astype(jnp.bfloat16), local_values[:, cols], preferred_element_type=jnp.float32
        ) + upper_sum[:, cols]
        merged.append((None, total, weighted))
    return merged


def solution(mesh):
    in_specs = (
        P("tok", "grp"),
        P("tok", "grp"),
        P("tok", "grp"),
        P("tok", "grp"),
        P("grp", None),
        P("tok", None, "grp"),
        P("tok", None, "grp"),
        P(None, "tok", "grp"),
        P(None, "tok", "grp"),
        P(),
        P(),
        P(),
        P(),
        P(),
    )
    out_specs = P("tok", "grp")
    return jax.shard_map(shards, mesh=mesh, in_specs=in_specs, out_specs=out_specs, check_vma=False)
```

```python
import jax
import jax.numpy as jnp
from jax import lax
from jax.experimental import pallas as pl
from jax.experimental.pallas import tpu as pltpu
from jax.sharding import PartitionSpec as P

HEAD_DIM = 128


NEG_FILL = -1e30


def partial_attention(query_rows, key_rows, values, allowed, head_count):
    head_width = query_rows.shape[1] // head_count
    parts = []
    for head in range(head_count):
        cols = slice(head * head_width, (head + 1) * head_width)
        scores = lax.dot_general(
            query_rows[:, cols],
            key_rows[:, cols],
            (((1,), (1,)), ((), ())),
            preferred_element_type=jnp.float32,
        ) * head_width ** (-0.5)
        scores = jnp.where(allowed, scores, NEG_FILL)
        row_max = jnp.max(scores, axis=1, keepdims=True)
        exp_scores = jnp.where(allowed, jnp.exp(scores - row_max), 0.0)
        row_total = jnp.sum(exp_scores, axis=1, keepdims=True)
        weighted = jnp.dot(
            exp_scores.astype(jnp.bfloat16),
            values[:, cols],
            preferred_element_type=jnp.float32,
        )
        parts.append((row_max, row_total, weighted))
    return parts


def combine(earlier, latter):
    merged = []
    for (max_a, total_a, sum_a), (max_b, total_b, sum_b) in zip(earlier, latter):
        new_max = jnp.maximum(max_a, max_b)
        scale_a = jnp.exp(max_a - new_max)
        scale_b = jnp.exp(max_b - new_max)
        merged.append(
            (new_max, total_a * scale_a + total_b * scale_b, sum_a * scale_a + sum_b * scale_b)
        )
    return merged


def gather_nodes(dest_nodes, upper_keys, upper_values):
    dest_count = dest_nodes.shape[0]
    chunk, cols = upper_keys.shape[1], upper_keys.shape[2]

    def kernel(nodes_ref, keys_ref, values_ref, out_ref, sems):
        def copies(dest):
            found = []
            for slot in range(2):
                node = nodes_ref[dest, slot]
                found.append(
                    pltpu.make_async_copy(
                        keys_ref.at[node], out_ref.at[dest, slot], sems.at[dest, slot]
                    )
                )
                found.append(
                    pltpu.make_async_copy(
                        values_ref.at[node], out_ref.at[dest, 2 + slot], sems.at[dest, 2 + slot]
                    )
                )
            return found

        def start(dest, carry):
            for copy in copies(dest):
                copy.start()
            return carry

        def wait(dest, carry):
            for copy in copies(dest):
                copy.wait()
            return carry

        lax.fori_loop(0, dest_count, start, 0)
        lax.fori_loop(0, dest_count, wait, 0)

    return pl.pallas_call(
        kernel,
        out_shape=jax.ShapeDtypeStruct((dest_count, 4, chunk, cols), upper_keys.dtype),
        grid_spec=pltpu.PrefetchScalarGridSpec(
            num_scalar_prefetch=1,
            grid=(1,),
            in_specs=[pl.BlockSpec(memory_space=pl.ANY), pl.BlockSpec(memory_space=pl.ANY)],
            out_specs=pl.BlockSpec(memory_space=pl.ANY),
            scratch_shapes=[pltpu.SemaphoreType.DMA((dest_count, 4))],
        ),
    )(dest_nodes, upper_keys, upper_values)


def sum_over_grp(projected):
    size = lax.axis_size("grp")
    index = lax.axis_index("grp")
    block = projected.shape[1] // size
    kept = projected
    step = size // 2
    while step >= 1:
        width = step * block
        lower = (index & step) == 0
        keep = jnp.where(lower, kept[:, :width], kept[:, width:])
        give = jnp.where(lower, kept[:, width:], kept[:, :width])
        if step == size // 2:
            give = give.astype(jnp.bfloat16)
        pairs = [(g, g ^ step) for g in range(size)]
        kept = keep + lax.ppermute(give, "grp", pairs).astype(jnp.float32)
        step //= 2
    return kept


def shards(
    queries,
    new_keys,
    new_values,
    residual,
    w_out,
    leaf_keys,
    leaf_values,
    upper_keys,
    upper_values,
    req_len,
    leaf_mid,
    mid_root,
    upper_len,
    leaf_len,
):
    dev_count = lax.axis_size("tok")
    my_index = lax.axis_index("tok")
    row_count = queries.shape[0]
    col_count = queries.shape[1]
    head_count = col_count // HEAD_DIM
    mid_count = mid_root.shape[0]
    node_count = upper_len.shape[0]
    root_count = node_count - mid_count
    chunk = upper_keys.shape[1]

    dest_mid = leaf_mid.astype(jnp.int32)
    dest_root = jnp.take(mid_root, dest_mid).astype(jnp.int32)
    dest_nodes = jnp.stack([dest_root, root_count + dest_mid], axis=1)
    send = gather_nodes(dest_nodes, upper_keys, upper_values)
    received = lax.all_to_all(send, "tok", 0, 0, tiled=True)
    recv_keys = received[:, :2]
    recv_values = received[:, 2:]

    owned = (jnp.arange(dev_count, dtype=jnp.int32) == my_index).astype(jnp.int32)
    my_length = jnp.sum(owned * req_len)
    my_mid = jnp.sum(owned * leaf_mid)
    my_leaf_len = jnp.sum(owned * leaf_len)
    my_root = jnp.sum((jnp.arange(mid_count) == my_mid).astype(jnp.int32) * mid_root)
    node_ids = jnp.arange(node_count)
    root_len = jnp.sum((node_ids == my_root).astype(jnp.int32) * upper_len)
    mid_len = jnp.sum((node_ids == root_count + my_mid).astype(jnp.int32) * upper_len)
    position = jnp.arange(row_count, dtype=jnp.int32)
    is_live = position < my_length
    leaf_count = leaf_keys.shape[1]
    local_keys = jnp.concatenate([leaf_keys[0], new_keys], axis=0)
    local_values = jnp.concatenate([leaf_values[0], new_values], axis=0)
    leaf_allowed = jnp.broadcast_to(
        (jnp.arange(leaf_count) < my_leaf_len)[None, :], (row_count, leaf_count)
    )
    new_allowed = (position[None, :] <= position[:, None]) & is_live[None, :]
    local_part = partial_attention(
        queries,
        local_keys,
        local_values,
        jnp.concatenate([leaf_allowed, new_allowed], axis=1),
        head_count,
    )

    upper_pos = (
        jnp.arange(dev_count, dtype=jnp.int32)[:, None, None] * chunk
        + jnp.arange(chunk, dtype=jnp.int32)[None, None, :]
    )
    upper_limit = jnp.stack([root_len, mid_len])[None, :, None]
    upper_ok = (upper_pos < upper_limit).reshape(-1)
    upper_part = partial_attention(
        queries,
        recv_keys.reshape(-1, col_count),
        recv_values.reshape(-1, col_count),
        upper_ok[None, :],
        head_count,
    )
    merged = combine(local_part, upper_part)
    attended = jnp.concatenate([part[2] / part[1] for part in merged], axis=1)
    attention = jnp.where(is_live[:, None], attended, 0.0).astype(jnp.bfloat16)
    projected = jnp.dot(attention, w_out, preferred_element_type=jnp.float32)
    mixed = sum_over_grp(projected)
    return (residual.astype(jnp.float32) + mixed).astype(jnp.bfloat16)


def solution(mesh):
    in_specs = (
        P("tok", "grp"),
        P("tok", "grp"),
        P("tok", "grp"),
        P("tok", "grp"),
        P("grp", None),
        P("tok", None, "grp"),
        P("tok", None, "grp"),
        P(None, "tok", "grp"),
        P(None, "tok", "grp"),
        P(),
        P(),
        P(),
        P(),
        P(),
    )
    out_specs = P("tok", "grp")
    return jax.shard_map(shards, mesh=mesh, in_specs=in_specs, out_specs=out_specs, check_vma=False)
```

```python
import jax
import jax.numpy as jnp
from jax import lax
from jax.sharding import PartitionSpec as P

HEAD_DIM = 128


NEG_FILL = -1e30


def partial_attention(query_rows, key_rows, values, allowed, head_count):
    head_width = query_rows.shape[1] // head_count
    parts = []
    for head in range(head_count):
        cols = slice(head * head_width, (head + 1) * head_width)
        scores = lax.dot_general(
            query_rows[:, cols],
            key_rows[:, cols],
            (((1,), (1,)), ((), ())),
            preferred_element_type=jnp.float32,
        ) * head_width ** (-0.5)
        scores = jnp.where(allowed, scores, NEG_FILL)
        row_max = jnp.max(scores, axis=1, keepdims=True)
        exp_scores = jnp.where(allowed, jnp.exp(scores - row_max), 0.0)
        row_total = jnp.sum(exp_scores, axis=1, keepdims=True)
        weighted = jnp.dot(
            exp_scores.astype(jnp.bfloat16),
            values[:, cols],
            preferred_element_type=jnp.float32,
        )
        parts.append((row_max, row_total, weighted))
    return parts


def combine(earlier, latter):
    merged = []
    for (max_a, total_a, sum_a), (max_b, total_b, sum_b) in zip(earlier, latter):
        new_max = jnp.maximum(max_a, max_b)
        scale_a = jnp.exp(max_a - new_max)
        scale_b = jnp.exp(max_b - new_max)
        merged.append(
            (new_max, total_a * scale_a + total_b * scale_b, sum_a * scale_a + sum_b * scale_b)
        )
    return merged


def sum_over_grp(projected):
    size = lax.axis_size("grp")
    index = lax.axis_index("grp")
    block = projected.shape[1] // size
    kept = projected
    step = size // 2
    while step >= 1:
        width = step * block
        lower = (index & step) == 0
        keep = jnp.where(lower, kept[:, :width], kept[:, width:])
        give = jnp.where(lower, kept[:, width:], kept[:, :width])
        if step == size // 2:
            give = give.astype(jnp.bfloat16)
        pairs = [(g, g ^ step) for g in range(size)]
        kept = keep + lax.ppermute(give, "grp", pairs).astype(jnp.float32)
        step //= 2
    return kept


def shards(
    queries,
    new_keys,
    new_values,
    residual,
    w_out,
    leaf_keys,
    leaf_values,
    upper_keys,
    upper_values,
    req_len,
    leaf_mid,
    mid_root,
    upper_len,
    leaf_len,
):
    dev_count = lax.axis_size("tok")
    my_index = lax.axis_index("tok")
    row_count = queries.shape[0]
    col_count = queries.shape[1]
    head_count = col_count // HEAD_DIM
    mid_count = mid_root.shape[0]
    node_count = upper_len.shape[0]
    root_count = node_count - mid_count
    chunk = upper_keys.shape[1]

    dest_mid = leaf_mid.astype(jnp.int32)
    dest_root = jnp.take(mid_root, dest_mid).astype(jnp.int32)
    dest_nodes = jnp.stack([dest_root, root_count + dest_mid], axis=1)
    both = jnp.concatenate([upper_keys, upper_values], axis=0)
    send = both.at[jnp.concatenate([dest_nodes, node_count + dest_nodes], axis=1)].get(
        mode="promise_in_bounds"
    )
    received = lax.all_to_all(send, "tok", 0, 0, tiled=True)
    recv_keys = received[:, :2]
    recv_values = received[:, 2:]

    owned = (jnp.arange(dev_count, dtype=jnp.int32) == my_index).astype(jnp.int32)
    my_length = jnp.sum(owned * req_len)
    my_mid = jnp.sum(owned * leaf_mid)
    my_leaf_len = jnp.sum(owned * leaf_len)
    my_root = jnp.sum((jnp.arange(mid_count) == my_mid).astype(jnp.int32) * mid_root)
    node_ids = jnp.arange(node_count)
    root_len = jnp.sum((node_ids == my_root).astype(jnp.int32) * upper_len)
    mid_len = jnp.sum((node_ids == root_count + my_mid).astype(jnp.int32) * upper_len)
    position = jnp.arange(row_count, dtype=jnp.int32)
    is_live = position < my_length
    leaf_count = leaf_keys.shape[1]
    local_keys = jnp.concatenate([leaf_keys[0], new_keys], axis=0)
    local_values = jnp.concatenate([leaf_values[0], new_values], axis=0)
    leaf_allowed = jnp.broadcast_to(
        (jnp.arange(leaf_count) < my_leaf_len)[None, :], (row_count, leaf_count)
    )
    new_allowed = (position[None, :] <= position[:, None]) & is_live[None, :]
    local_part = partial_attention(
        queries,
        local_keys,
        local_values,
        jnp.concatenate([leaf_allowed, new_allowed], axis=1),
        head_count,
    )

    upper_pos = (
        jnp.arange(dev_count, dtype=jnp.int32)[:, None, None] * chunk
        + jnp.arange(chunk, dtype=jnp.int32)[None, None, :]
    )
    upper_limit = jnp.stack([root_len, mid_len])[None, :, None]
    upper_ok = (upper_pos < upper_limit).reshape(-1)
    upper_part = partial_attention(
        queries,
        recv_keys.reshape(-1, col_count),
        recv_values.reshape(-1, col_count),
        upper_ok[None, :],
        head_count,
    )
    merged = combine(local_part, upper_part)
    attended = jnp.concatenate([part[2] / part[1] for part in merged], axis=1)
    attention = jnp.where(is_live[:, None], attended, 0.0).astype(jnp.bfloat16)
    projected = jnp.dot(attention, w_out, preferred_element_type=jnp.float32)
    mixed = sum_over_grp(projected)
    return (residual.astype(jnp.float32) + mixed).astype(jnp.bfloat16)


def solution(mesh):
    in_specs = (
        P("tok", "grp"),
        P("tok", "grp"),
        P("tok", "grp"),
        P("tok", "grp"),
        P("grp", None),
        P("tok", None, "grp"),
        P("tok", None, "grp"),
        P(None, "tok", "grp"),
        P(None, "tok", "grp"),
        P(),
        P(),
        P(),
        P(),
        P(),
    )
    out_specs = P("tok", "grp")
    return jax.shard_map(shards, mesh=mesh, in_specs=in_specs, out_specs=out_specs, check_vma=False)
```

```python
import jax
import jax.numpy as jnp
from jax import lax
from jax.sharding import PartitionSpec as P

HEAD_DIM = 128


NEG_FILL = -1e30


def partial_attention(query_rows, key_rows, values, allowed, head_count):
    head_width = query_rows.shape[1] // head_count
    parts = []
    for head in range(head_count):
        cols = slice(head * head_width, (head + 1) * head_width)
        scores = lax.dot_general(
            query_rows[:, cols],
            key_rows[:, cols],
            (((1,), (1,)), ((), ())),
            preferred_element_type=jnp.float32,
        ) * head_width ** (-0.5)
        scores = jnp.where(allowed, scores, NEG_FILL)
        row_max = jnp.max(scores, axis=1, keepdims=True)
        exp_scores = jnp.where(allowed, jnp.exp(scores - row_max), 0.0)
        row_total = jnp.sum(exp_scores, axis=1, keepdims=True)
        weighted = jnp.dot(
            exp_scores.astype(jnp.bfloat16),
            values[:, cols],
            preferred_element_type=jnp.float32,
        )
        parts.append((row_max, row_total, weighted))
    return parts


def combine(earlier, latter):
    merged = []
    for (max_a, total_a, sum_a), (max_b, total_b, sum_b) in zip(earlier, latter):
        new_max = jnp.maximum(max_a, max_b)
        scale_a = jnp.exp(max_a - new_max)
        scale_b = jnp.exp(max_b - new_max)
        merged.append(
            (new_max, total_a * scale_a + total_b * scale_b, sum_a * scale_a + sum_b * scale_b)
        )
    return merged


def sum_over_grp(projected):
    size = lax.axis_size("grp")
    index = lax.axis_index("grp")
    rows = projected.shape[0]
    block = projected.shape[1] // size
    kept = projected.reshape(rows, size, block)
    step = 1
    while step < size:
        pairs = kept.reshape(rows, kept.shape[1] // 2, 2, block)
        high = (index & step) != 0
        keep = jnp.where(high, pairs[:, :, 1], pairs[:, :, 0])
        give = jnp.where(high, pairs[:, :, 0], pairs[:, :, 1])
        if step * 2 == size:
            give = give.astype(jnp.bfloat16)
        moved = lax.ppermute(give, "grp", [(g, g ^ step) for g in range(size)])
        kept = keep + moved.astype(jnp.float32)
        step *= 2
    return kept.reshape(rows, block)


def pick(table, index):
    ids = jnp.arange(table.shape[0], dtype=jnp.int32)
    return jnp.sum(jnp.where(ids == index, table, 0))


def shards(
    queries,
    new_keys,
    new_values,
    residual,
    w_out,
    leaf_keys,
    leaf_values,
    upper_keys,
    upper_values,
    req_len,
    leaf_mid,
    mid_root,
    upper_len,
    leaf_len,
):
    dev_count = lax.axis_size("tok")
    my_index = lax.axis_index("tok")
    row_count = queries.shape[0]
    col_count = queries.shape[1]
    head_count = col_count // HEAD_DIM
    mid_count = mid_root.shape[0]
    node_count = upper_len.shape[0]
    root_count = node_count - mid_count
    chunk = upper_keys.shape[1]

    root_rows = jnp.stack([upper_keys[:root_count], upper_values[:root_count]], axis=1)
    roots = lax.all_gather(root_rows[None], "tok", axis=0, tiled=True)
    dest_mid = root_count + leaf_mid.astype(jnp.int32)
    mid_rows = jnp.concatenate([upper_keys, upper_values], axis=0)
    send = mid_rows.at[jnp.stack([dest_mid, node_count + dest_mid], axis=1)].get(
        mode="promise_in_bounds"
    )
    mids = lax.all_to_all(send, "tok", 0, 0, tiled=True)

    my_length = pick(req_len, my_index)
    my_mid = pick(leaf_mid, my_index)
    my_leaf_len = pick(leaf_len, my_index)
    my_root = pick(mid_root, my_mid)
    root_len = pick(upper_len, my_root)
    mid_len = pick(upper_len, root_count + my_mid)
    position = jnp.arange(row_count, dtype=jnp.int32)
    is_live = position < my_length
    leaf_count = leaf_keys.shape[1]
    local_keys = jnp.concatenate([leaf_keys[0], new_keys], axis=0)
    local_values = jnp.concatenate([leaf_values[0], new_values], axis=0)
    leaf_allowed = jnp.broadcast_to(
        (jnp.arange(leaf_count) < my_leaf_len)[None, :], (row_count, leaf_count)
    )
    new_allowed = (position[None, :] <= position[:, None]) & is_live[None, :]
    merged = partial_attention(
        queries,
        local_keys,
        local_values,
        jnp.concatenate([leaf_allowed, new_allowed], axis=1),
        head_count,
    )

    upper_pos = (
        jnp.arange(dev_count, dtype=jnp.int32)[:, None] * chunk
        + jnp.arange(chunk, dtype=jnp.int32)[None, :]
    ).reshape(-1)
    my_roots = lax.dynamic_index_in_dim(roots, my_root, axis=1, keepdims=False)
    root_part = partial_attention(
        queries,
        my_roots[:, 0].reshape(-1, col_count),
        my_roots[:, 1].reshape(-1, col_count),
        (upper_pos < root_len)[None, :],
        head_count,
    )
    merged = combine(merged, root_part)
    mid_part = partial_attention(
        queries,
        mids[:, 0].reshape(-1, col_count),
        mids[:, 1].reshape(-1, col_count),
        (upper_pos < mid_len)[None, :],
        head_count,
    )
    merged = combine(merged, mid_part)
    attended = jnp.concatenate([part[2] / part[1] for part in merged], axis=1)
    attention = jnp.where(is_live[:, None], attended, 0.0).astype(jnp.bfloat16)
    projected = jnp.dot(attention, w_out, preferred_element_type=jnp.float32)
    mixed = sum_over_grp(projected)
    return (residual.astype(jnp.float32) + mixed).astype(jnp.bfloat16)


def solution(mesh):
    in_specs = (
        P("tok", "grp"),
        P("tok", "grp"),
        P("tok", "grp"),
        P("tok", "grp"),
        P("grp", None),
        P("tok", None, "grp"),
        P("tok", None, "grp"),
        P(None, "tok", "grp"),
        P(None, "tok", "grp"),
        P(),
        P(),
        P(),
        P(),
        P(),
    )
    out_specs = P("tok", "grp")
    return jax.shard_map(shards, mesh=mesh, in_specs=in_specs, out_specs=out_specs, check_vma=False)
```

```python
import jax
import jax.numpy as jnp
from jax import lax
from jax.sharding import PartitionSpec as P

HEAD_DIM = 128


NEG_FILL = -1e30


def partial_attention(query_rows, key_rows, values, allowed, head_count):
    head_width = query_rows.shape[1] // head_count
    parts = []
    for head in range(head_count):
        cols = slice(head * head_width, (head + 1) * head_width)
        scores = lax.dot_general(
            query_rows[:, cols],
            key_rows[:, cols],
            (((1,), (1,)), ((), ())),
            preferred_element_type=jnp.float32,
        ) * head_width ** (-0.5)
        scores = jnp.where(allowed, scores, NEG_FILL)
        row_max = jnp.max(scores, axis=1, keepdims=True)
        exp_scores = jnp.where(allowed, jnp.exp(scores - row_max), 0.0)
        row_total = jnp.sum(exp_scores, axis=1, keepdims=True)
        weighted = jnp.dot(
            exp_scores.astype(jnp.bfloat16),
            values[:, cols],
            preferred_element_type=jnp.float32,
        )
        parts.append((row_max, row_total, weighted))
    return parts


def combine(earlier, latter):
    merged = []
    for (max_a, total_a, sum_a), (max_b, total_b, sum_b) in zip(earlier, latter):
        new_max = jnp.maximum(max_a, max_b)
        scale_a = jnp.exp(max_a - new_max)
        scale_b = jnp.exp(max_b - new_max)
        merged.append(
            (new_max, total_a * scale_a + total_b * scale_b, sum_a * scale_a + sum_b * scale_b)
        )
    return merged


def sum_over_grp(projected):
    size = lax.axis_size("grp")
    index = lax.axis_index("grp")
    rows = projected.shape[0]
    block = projected.shape[1] // size
    kept = projected.reshape(rows, size, block)
    step = 1
    while step < size:
        pairs = kept.reshape(rows, kept.shape[1] // 2, 2, block)
        high = (index & step) != 0
        keep = jnp.where(high, pairs[:, :, 1], pairs[:, :, 0])
        give = jnp.where(high, pairs[:, :, 0], pairs[:, :, 1])
        if step * 2 == size:
            give = give.astype(jnp.bfloat16)
        moved = lax.ppermute(give, "grp", [(g, g ^ step) for g in range(size)])
        kept = keep + moved.astype(jnp.float32)
        step *= 2
    return kept.reshape(rows, block)


def pick(table, index):
    ids = jnp.arange(table.shape[0], dtype=jnp.int32)
    return jnp.sum(jnp.where(ids == index, table, 0))


def shards(
    queries,
    new_keys,
    new_values,
    residual,
    w_out,
    leaf_keys,
    leaf_values,
    upper_keys,
    upper_values,
    req_len,
    leaf_mid,
    mid_root,
    upper_len,
    leaf_len,
):
    dev_count = lax.axis_size("tok")
    my_index = lax.axis_index("tok")
    row_count = queries.shape[0]
    col_count = queries.shape[1]
    head_count = col_count // HEAD_DIM
    mid_count = mid_root.shape[0]
    node_count = upper_len.shape[0]
    root_count = node_count - mid_count
    chunk = upper_keys.shape[1]

    dest_mid = leaf_mid.astype(jnp.int32)
    mid_ids = jnp.arange(mid_count, dtype=jnp.int32)
    dest_root = jnp.sum(
        jnp.where(dest_mid[:, None] == mid_ids[None, :], mid_root[None, :], 0), axis=1
    )
    dest_nodes = jnp.stack([dest_root, root_count + dest_mid], axis=1)
    both = jnp.concatenate([upper_keys, upper_values], axis=0)
    send = both.at[jnp.concatenate([dest_nodes, node_count + dest_nodes], axis=1)].get(
        mode="promise_in_bounds"
    )
    received = lax.all_to_all(send, "tok", 0, 0, tiled=True)
    recv_keys = received[:, :2]
    recv_values = received[:, 2:]

    my_length = pick(req_len, my_index)
    my_mid = pick(leaf_mid, my_index)
    my_leaf_len = pick(leaf_len, my_index)
    my_root = pick(mid_root, my_mid)
    root_len = pick(upper_len, my_root)
    mid_len = pick(upper_len, root_count + my_mid)
    position = jnp.arange(row_count, dtype=jnp.int32)
    is_live = position < my_length
    leaf_count = leaf_keys.shape[1]
    local_keys = jnp.concatenate([leaf_keys[0], new_keys], axis=0)
    local_values = jnp.concatenate([leaf_values[0], new_values], axis=0)
    leaf_allowed = jnp.broadcast_to(
        (jnp.arange(leaf_count) < my_leaf_len)[None, :], (row_count, leaf_count)
    )
    new_allowed = (position[None, :] <= position[:, None]) & is_live[None, :]
    local_part = partial_attention(
        queries,
        local_keys,
        local_values,
        jnp.concatenate([leaf_allowed, new_allowed], axis=1),
        head_count,
    )

    upper_pos = (
        jnp.arange(dev_count, dtype=jnp.int32)[:, None, None] * chunk
        + jnp.arange(chunk, dtype=jnp.int32)[None, None, :]
    )
    upper_limit = jnp.stack([root_len, mid_len])[None, :, None]
    upper_ok = (upper_pos < upper_limit).reshape(-1)
    upper_part = partial_attention(
        queries,
        recv_keys.reshape(-1, col_count),
        recv_values.reshape(-1, col_count),
        upper_ok[None, :],
        head_count,
    )
    merged = combine(local_part, upper_part)
    attended = jnp.concatenate([part[2] / part[1] for part in merged], axis=1)
    attention = jnp.where(is_live[:, None], attended, 0.0).astype(jnp.bfloat16)
    projected = jnp.dot(attention, w_out, preferred_element_type=jnp.float32)
    mixed = sum_over_grp(projected)
    return (residual.astype(jnp.float32) + mixed).astype(jnp.bfloat16)


def solution(mesh):
    in_specs = (
        P("tok", "grp"),
        P("tok", "grp"),
        P("tok", "grp"),
        P("tok", "grp"),
        P("grp", None),
        P("tok", None, "grp"),
        P("tok", None, "grp"),
        P(None, "tok", "grp"),
        P(None, "tok", "grp"),
        P(),
        P(),
        P(),
        P(),
        P(),
    )
    out_specs = P("tok", "grp")
    return jax.shard_map(shards, mesh=mesh, in_specs=in_specs, out_specs=out_specs, check_vma=False)
```

```python
import jax
import jax.numpy as jnp
from jax import lax
from jax.sharding import PartitionSpec as P

HEAD_DIM = 128


NEG_FILL = -1e30


def partial_attention(query_rows, key_rows, values, allowed, head_count):
    head_width = query_rows.shape[1] // head_count
    parts = []
    for head in range(head_count):
        cols = slice(head * head_width, (head + 1) * head_width)
        scores = lax.dot_general(
            query_rows[:, cols],
            key_rows[:, cols],
            (((1,), (1,)), ((), ())),
            preferred_element_type=jnp.float32,
        ) * head_width ** (-0.5)
        scores = jnp.where(allowed, scores, NEG_FILL)
        row_max = jnp.max(scores, axis=1, keepdims=True)
        exp_scores = jnp.where(allowed, jnp.exp(scores - row_max), 0.0)
        row_total = jnp.sum(exp_scores, axis=1, keepdims=True)
        weighted = jnp.dot(
            exp_scores.astype(jnp.bfloat16),
            values[:, cols],
            preferred_element_type=jnp.float32,
        )
        parts.append((row_max, row_total, weighted))
    return parts


def combine(earlier, latter):
    merged = []
    for (max_a, total_a, sum_a), (max_b, total_b, sum_b) in zip(earlier, latter):
        new_max = jnp.maximum(max_a, max_b)
        scale_a = jnp.exp(max_a - new_max)
        scale_b = jnp.exp(max_b - new_max)
        merged.append(
            (new_max, total_a * scale_a + total_b * scale_b, sum_a * scale_a + sum_b * scale_b)
        )
    return merged


def project_over_grp(attention, w_out):
    size = lax.axis_size("grp")
    index = lax.axis_index("grp")
    block = w_out.shape[1] // size
    kept = [
        jnp.dot(attention, w_out[:, b * block : (b + 1) * block], preferred_element_type=jnp.float32)
        for b in range(size)
    ]
    step = 1
    while step < size:
        high = (index & step) != 0
        keep = [jnp.where(high, kept[k + 1], kept[k]) for k in range(0, len(kept), 2)]
        give = jnp.concatenate(
            [jnp.where(high, kept[k], kept[k + 1]) for k in range(0, len(kept), 2)], axis=1
        )
        if step * 2 == size:
            give = give.astype(jnp.bfloat16)
        moved = lax.ppermute(give, "grp", [(g, g ^ step) for g in range(size)]).astype(jnp.float32)
        kept = [part + moved[:, k * block : (k + 1) * block] for k, part in enumerate(keep)]
        step *= 2
    return kept[0]


def pick(table, index):
    ids = jnp.arange(table.shape[0], dtype=jnp.int32)
    return jnp.sum(jnp.where(ids == index, table, 0))


def shards(
    queries,
    new_keys,
    new_values,
    residual,
    w_out,
    leaf_keys,
    leaf_values,
    upper_keys,
    upper_values,
    req_len,
    leaf_mid,
    mid_root,
    upper_len,
    leaf_len,
):
    dev_count = lax.axis_size("tok")
    my_index = lax.axis_index("tok")
    row_count = queries.shape[0]
    col_count = queries.shape[1]
    head_count = col_count // HEAD_DIM
    mid_count = mid_root.shape[0]
    node_count = upper_len.shape[0]
    root_count = node_count - mid_count
    chunk = upper_keys.shape[1]

    dest_mid = leaf_mid.astype(jnp.int32)
    mid_ids = jnp.arange(mid_count, dtype=jnp.int32)
    dest_root = jnp.sum(
        jnp.where(dest_mid[:, None] == mid_ids[None, :], mid_root[None, :], 0), axis=1
    )
    dest_nodes = jnp.stack([dest_root, root_count + dest_mid], axis=1)
    both = jnp.concatenate([upper_keys, upper_values], axis=0)
    send = both.at[jnp.concatenate([dest_nodes, node_count + dest_nodes], axis=1)].get(
        mode="promise_in_bounds"
    )
    received = lax.all_to_all(send, "tok", 0, 0, tiled=True)
    recv_keys = received[:, :2]
    recv_values = received[:, 2:]

    my_length = pick(req_len, my_index)
    my_mid = pick(leaf_mid, my_index)
    my_leaf_len = pick(leaf_len, my_index)
    my_root = pick(mid_root, my_mid)
    root_len = pick(upper_len, my_root)
    mid_len = pick(upper_len, root_count + my_mid)
    position = jnp.arange(row_count, dtype=jnp.int32)
    is_live = position < my_length
    leaf_count = leaf_keys.shape[1]
    local_keys = jnp.concatenate([leaf_keys[0], new_keys], axis=0)
    local_values = jnp.concatenate([leaf_values[0], new_values], axis=0)
    leaf_allowed = jnp.broadcast_to(
        (jnp.arange(leaf_count) < my_leaf_len)[None, :], (row_count, leaf_count)
    )
    new_allowed = (position[None, :] <= position[:, None]) & is_live[None, :]
    local_part = partial_attention(
        queries,
        local_keys,
        local_values,
        jnp.concatenate([leaf_allowed, new_allowed], axis=1),
        head_count,
    )

    upper_pos = (
        jnp.arange(dev_count, dtype=jnp.int32)[:, None, None] * chunk
        + jnp.arange(chunk, dtype=jnp.int32)[None, None, :]
    )
    upper_limit = jnp.stack([root_len, mid_len])[None, :, None]
    upper_ok = (upper_pos < upper_limit).reshape(-1)
    upper_part = partial_attention(
        queries,
        recv_keys.reshape(-1, col_count),
        recv_values.reshape(-1, col_count),
        upper_ok[None, :],
        head_count,
    )
    merged = combine(local_part, upper_part)
    attended = jnp.concatenate([part[2] / part[1] for part in merged], axis=1)
    attention = jnp.where(is_live[:, None], attended, 0.0).astype(jnp.bfloat16)
    mixed = project_over_grp(attention, w_out)
    return (residual.astype(jnp.float32) + mixed).astype(jnp.bfloat16)


def solution(mesh):
    in_specs = (
        P("tok", "grp"),
        P("tok", "grp"),
        P("tok", "grp"),
        P("tok", "grp"),
        P("grp", None),
        P("tok", None, "grp"),
        P("tok", None, "grp"),
        P(None, "tok", "grp"),
        P(None, "tok", "grp"),
        P(),
        P(),
        P(),
        P(),
        P(),
    )
    out_specs = P("tok", "grp")
    return jax.shard_map(shards, mesh=mesh, in_specs=in_specs, out_specs=out_specs, check_vma=False)
```

```python
import jax
import jax.numpy as jnp
from jax import lax
from jax.sharding import PartitionSpec as P

HEAD_DIM = 128


NEG_FILL = -1e30


def partial_attention(query_rows, key_rows, values, allowed, head_count):
    head_width = query_rows.shape[1] // head_count
    parts = []
    for head in range(head_count):
        cols = slice(head * head_width, (head + 1) * head_width)
        scores = lax.dot_general(
            query_rows[:, cols],
            key_rows[:, cols],
            (((1,), (1,)), ((), ())),
            preferred_element_type=jnp.float32,
        ) * head_width ** (-0.5)
        scores = jnp.where(allowed, scores, NEG_FILL)
        row_max = jnp.max(scores, axis=1, keepdims=True)
        exp_scores = jnp.where(allowed, jnp.exp(scores - row_max), 0.0)
        row_total = jnp.sum(exp_scores, axis=1, keepdims=True)
        weighted = jnp.dot(
            exp_scores.astype(jnp.bfloat16),
            values[:, cols],
            preferred_element_type=jnp.float32,
        )
        parts.append((row_max, row_total, weighted))
    return parts


def combine(earlier, latter):
    merged = []
    for (max_a, total_a, sum_a), (max_b, total_b, sum_b) in zip(earlier, latter):
        new_max = jnp.maximum(max_a, max_b)
        scale_a = jnp.exp(max_a - new_max)
        scale_b = jnp.exp(max_b - new_max)
        merged.append(
            (new_max, total_a * scale_a + total_b * scale_b, sum_a * scale_a + sum_b * scale_b)
        )
    return merged


def project_over_grp(attention, w_out):
    size = lax.axis_size("grp")
    index = lax.axis_index("grp")
    block = w_out.shape[1] // size
    kept = [
        jnp.dot(attention, w_out[:, b * block : (b + 1) * block], preferred_element_type=jnp.float32)
        for b in range(size)
    ]
    step = 1
    while step < size:
        high = (index & step) != 0
        keep = [jnp.where(high, kept[k + 1], kept[k]) for k in range(0, len(kept), 2)]
        give = jnp.concatenate(
            [jnp.where(high, kept[k], kept[k + 1]) for k in range(0, len(kept), 2)], axis=1
        )
        if step * 2 == size:
            give = give.astype(jnp.bfloat16)
        moved = lax.ppermute(give, "grp", [(g, g ^ step) for g in range(size)]).astype(jnp.float32)
        kept = [part + moved[:, k * block : (k + 1) * block] for k, part in enumerate(keep)]
        step *= 2
    return kept[0]


def pick(table, index):
    ids = jnp.arange(table.shape[0], dtype=jnp.int32)
    return jnp.sum(jnp.where(ids == index, table, 0))


def shards(
    queries,
    new_keys,
    new_values,
    residual,
    w_out,
    leaf_keys,
    leaf_values,
    upper_keys,
    upper_values,
    req_len,
    leaf_mid,
    mid_root,
    upper_len,
    leaf_len,
):
    dev_count = lax.axis_size("tok")
    my_index = lax.axis_index("tok")
    row_count = queries.shape[0]
    col_count = queries.shape[1]
    head_count = col_count // HEAD_DIM
    mid_count = mid_root.shape[0]
    node_count = upper_len.shape[0]
    root_count = node_count - mid_count
    chunk = upper_keys.shape[1]

    dest_mid = leaf_mid.astype(jnp.int32)
    mid_ids = jnp.arange(mid_count, dtype=jnp.int32)
    dest_root = jnp.sum(
        jnp.where(dest_mid[:, None] == mid_ids[None, :], mid_root[None, :], 0), axis=1
    )
    dest_nodes = jnp.stack([dest_root, root_count + dest_mid], axis=1)
    both = jnp.concatenate([upper_keys, upper_values], axis=0)
    both_nodes = jnp.concatenate([dest_nodes, node_count + dest_nodes], axis=1)
    if dev_count <= 8:
        shift = jnp.arange(dev_count, dtype=jnp.int32)
        order = (my_index + shift) % dev_count
        slabs = both.at[both_nodes[order]].get(mode="promise_in_bounds")
        received = [slabs[0]] + [
            lax.ppermute(slabs[k], "tok", [(j, (j + k) % dev_count) for j in range(dev_count)])
            for k in range(1, dev_count)
        ]
        received = jnp.stack(received)
        sources = (my_index - shift) % dev_count
    else:
        send = both.at[both_nodes].get(mode="promise_in_bounds")
        received = lax.all_to_all(send, "tok", 0, 0, tiled=True)
        sources = jnp.arange(dev_count, dtype=jnp.int32)
    recv_keys = received[:, :2]
    recv_values = received[:, 2:]

    my_length = pick(req_len, my_index)
    my_mid = pick(leaf_mid, my_index)
    my_leaf_len = pick(leaf_len, my_index)
    my_root = pick(mid_root, my_mid)
    root_len = pick(upper_len, my_root)
    mid_len = pick(upper_len, root_count + my_mid)
    position = jnp.arange(row_count, dtype=jnp.int32)
    is_live = position < my_length
    leaf_count = leaf_keys.shape[1]
    local_keys = jnp.concatenate([leaf_keys[0], new_keys], axis=0)
    local_values = jnp.concatenate([leaf_values[0], new_values], axis=0)
    leaf_allowed = jnp.broadcast_to(
        (jnp.arange(leaf_count) < my_leaf_len)[None, :], (row_count, leaf_count)
    )
    new_allowed = (position[None, :] <= position[:, None]) & is_live[None, :]
    local_part = partial_attention(
        queries,
        local_keys,
        local_values,
        jnp.concatenate([leaf_allowed, new_allowed], axis=1),
        head_count,
    )

    upper_pos = (
        sources[:, None, None] * chunk
        + jnp.arange(chunk, dtype=jnp.int32)[None, None, :]
    )
    upper_limit = jnp.stack([root_len, mid_len])[None, :, None]
    upper_ok = (upper_pos < upper_limit).reshape(-1)
    upper_part = partial_attention(
        queries,
        recv_keys.reshape(-1, col_count),
        recv_values.reshape(-1, col_count),
        upper_ok[None, :],
        head_count,
    )
    merged = combine(local_part, upper_part)
    attended = jnp.concatenate([part[2] / part[1] for part in merged], axis=1)
    attention = jnp.where(is_live[:, None], attended, 0.0).astype(jnp.bfloat16)
    mixed = project_over_grp(attention, w_out)
    return (residual.astype(jnp.float32) + mixed).astype(jnp.bfloat16)


def solution(mesh):
    in_specs = (
        P("tok", "grp"),
        P("tok", "grp"),
        P("tok", "grp"),
        P("tok", "grp"),
        P("grp", None),
        P("tok", None, "grp"),
        P("tok", None, "grp"),
        P(None, "tok", "grp"),
        P(None, "tok", "grp"),
        P(),
        P(),
        P(),
        P(),
        P(),
    )
    out_specs = P("tok", "grp")
    return jax.shard_map(shards, mesh=mesh, in_specs=in_specs, out_specs=out_specs, check_vma=False)
```

```python
import jax
import jax.numpy as jnp
from jax import lax
from jax.sharding import PartitionSpec as P

HEAD_DIM = 128


NEG_FILL = -1e30


def partial_attention(query_rows, key_rows, values, allowed, head_count):
    head_width = query_rows.shape[1] // head_count
    parts = []
    for head in range(head_count):
        cols = slice(head * head_width, (head + 1) * head_width)
        scores = lax.dot_general(
            query_rows[:, cols],
            key_rows[:, cols],
            (((1,), (1,)), ((), ())),
            preferred_element_type=jnp.float32,
        ) * head_width ** (-0.5)
        scores = jnp.where(allowed, scores, NEG_FILL)
        row_max = jnp.max(scores, axis=1, keepdims=True)
        exp_scores = jnp.where(allowed, jnp.exp(scores - row_max), 0.0)
        row_total = jnp.sum(exp_scores, axis=1, keepdims=True)
        weighted = jnp.dot(
            exp_scores.astype(jnp.bfloat16),
            values[:, cols],
            preferred_element_type=jnp.float32,
        )
        parts.append((row_max, row_total, weighted))
    return parts


def combine(earlier, latter):
    merged = []
    for (max_a, total_a, sum_a), (max_b, total_b, sum_b) in zip(earlier, latter):
        new_max = jnp.maximum(max_a, max_b)
        scale_a = jnp.exp(max_a - new_max)
        scale_b = jnp.exp(max_b - new_max)
        merged.append(
            (new_max, total_a * scale_a + total_b * scale_b, sum_a * scale_a + sum_b * scale_b)
        )
    return merged


def project_over_grp(attention, w_out):
    size = lax.axis_size("grp")
    index = lax.axis_index("grp")
    block = w_out.shape[1] // size
    kept = [
        jnp.dot(attention, w_out[:, b * block : (b + 1) * block], preferred_element_type=jnp.float32)
        for b in range(size)
    ]
    step = 1
    while step < size:
        high = (index & step) != 0
        keep = [jnp.where(high, kept[k + 1], kept[k]) for k in range(0, len(kept), 2)]
        give = jnp.concatenate(
            [jnp.where(high, kept[k], kept[k + 1]) for k in range(0, len(kept), 2)], axis=1
        )
        if step * 2 == size:
            give = give.astype(jnp.bfloat16)
        moved = lax.ppermute(give, "grp", [(g, g ^ step) for g in range(size)]).astype(jnp.float32)
        kept = [part + moved[:, k * block : (k + 1) * block] for k, part in enumerate(keep)]
        step *= 2
    return kept[0]


def pick(table, index):
    ids = jnp.arange(table.shape[0], dtype=jnp.int32)
    return jnp.sum(jnp.where(ids == index, table, 0))


def shards(
    queries,
    new_keys,
    new_values,
    residual,
    w_out,
    leaf_keys,
    leaf_values,
    upper_keys,
    upper_values,
    req_len,
    leaf_mid,
    mid_root,
    upper_len,
    leaf_len,
):
    dev_count = lax.axis_size("tok")
    my_index = lax.axis_index("tok")
    row_count = queries.shape[0]
    col_count = queries.shape[1]
    head_count = col_count // HEAD_DIM
    mid_count = mid_root.shape[0]
    node_count = upper_len.shape[0]
    root_count = node_count - mid_count
    chunk = upper_keys.shape[1]

    dest_mid = leaf_mid.astype(jnp.int32)
    mid_ids = jnp.arange(mid_count, dtype=jnp.int32)
    dest_root = jnp.sum(
        jnp.where(dest_mid[:, None] == mid_ids[None, :], mid_root[None, :], 0), axis=1
    )
    dest_nodes = jnp.stack([dest_root, root_count + dest_mid], axis=1)
    both = jnp.concatenate([upper_keys, upper_values], axis=0)
    both_nodes = jnp.concatenate([dest_nodes, node_count + dest_nodes], axis=1)
    if dev_count <= 8 and dev_count & (dev_count - 1) == 0:
        flips = jnp.arange(dev_count, dtype=jnp.int32)
        slabs = both.at[both_nodes[my_index ^ flips]].get(mode="promise_in_bounds")
        received = [None] * dev_count
        received[0] = slabs[0]
        for k in sorted(range(1, dev_count), key=lambda k: (-bin(k).count("1"), -k)):
            received[k] = lax.ppermute(slabs[k], "tok", [(j, j ^ k) for j in range(dev_count)])
        received = jnp.stack(received)
        sources = my_index ^ flips
    else:
        send = both.at[both_nodes].get(mode="promise_in_bounds")
        received = lax.all_to_all(send, "tok", 0, 0, tiled=True)
        sources = jnp.arange(dev_count, dtype=jnp.int32)
    recv_keys = received[:, :2]
    recv_values = received[:, 2:]

    my_length = pick(req_len, my_index)
    my_mid = pick(leaf_mid, my_index)
    my_leaf_len = pick(leaf_len, my_index)
    my_root = pick(mid_root, my_mid)
    root_len = pick(upper_len, my_root)
    mid_len = pick(upper_len, root_count + my_mid)
    position = jnp.arange(row_count, dtype=jnp.int32)
    is_live = position < my_length
    leaf_count = leaf_keys.shape[1]
    local_keys = jnp.concatenate([leaf_keys[0], new_keys], axis=0)
    local_values = jnp.concatenate([leaf_values[0], new_values], axis=0)
    leaf_allowed = jnp.broadcast_to(
        (jnp.arange(leaf_count) < my_leaf_len)[None, :], (row_count, leaf_count)
    )
    new_allowed = (position[None, :] <= position[:, None]) & is_live[None, :]
    local_part = partial_attention(
        queries,
        local_keys,
        local_values,
        jnp.concatenate([leaf_allowed, new_allowed], axis=1),
        head_count,
    )

    upper_pos = (
        sources[:, None, None] * chunk
        + jnp.arange(chunk, dtype=jnp.int32)[None, None, :]
    )
    upper_limit = jnp.stack([root_len, mid_len])[None, :, None]
    upper_ok = (upper_pos < upper_limit).reshape(-1)
    upper_part = partial_attention(
        queries,
        recv_keys.reshape(-1, col_count),
        recv_values.reshape(-1, col_count),
        upper_ok[None, :],
        head_count,
    )
    merged = combine(local_part, upper_part)
    attended = jnp.concatenate([part[2] / part[1] for part in merged], axis=1)
    attention = jnp.where(is_live[:, None], attended, 0.0).astype(jnp.bfloat16)
    mixed = project_over_grp(attention, w_out)
    return (residual.astype(jnp.float32) + mixed).astype(jnp.bfloat16)


def solution(mesh):
    in_specs = (
        P("tok", "grp"),
        P("tok", "grp"),
        P("tok", "grp"),
        P("tok", "grp"),
        P("grp", None),
        P("tok", None, "grp"),
        P("tok", None, "grp"),
        P(None, "tok", "grp"),
        P(None, "tok", "grp"),
        P(),
        P(),
        P(),
        P(),
        P(),
    )
    out_specs = P("tok", "grp")
    return jax.shard_map(shards, mesh=mesh, in_specs=in_specs, out_specs=out_specs, check_vma=False)
```

```python
import jax
import jax.numpy as jnp
from jax import lax
from jax.sharding import PartitionSpec as P

HEAD_DIM = 128


NEG_FILL = -1e30


def partial_attention(query_rows, key_rows, values, allowed, head_count):
    head_width = query_rows.shape[1] // head_count
    parts = []
    for head in range(head_count):
        cols = slice(head * head_width, (head + 1) * head_width)
        scores = lax.dot_general(
            query_rows[:, cols],
            key_rows[:, cols],
            (((1,), (1,)), ((), ())),
            preferred_element_type=jnp.float32,
        ) * head_width ** (-0.5)
        scores = jnp.where(allowed, scores, NEG_FILL)
        row_max = jnp.max(scores, axis=1, keepdims=True)
        exp_scores = jnp.where(allowed, jnp.exp(scores - row_max), 0.0)
        row_total = jnp.sum(exp_scores, axis=1, keepdims=True)
        weighted = jnp.dot(
            exp_scores.astype(jnp.bfloat16),
            values[:, cols],
            preferred_element_type=jnp.float32,
        )
        parts.append((row_max, row_total, weighted))
    return parts


def combine(earlier, latter):
    merged = []
    for (max_a, total_a, sum_a), (max_b, total_b, sum_b) in zip(earlier, latter):
        new_max = jnp.maximum(max_a, max_b)
        scale_a = jnp.exp(max_a - new_max)
        scale_b = jnp.exp(max_b - new_max)
        merged.append(
            (new_max, total_a * scale_a + total_b * scale_b, sum_a * scale_a + sum_b * scale_b)
        )
    return merged


def project_over_grp(attention, w_out):
    size = lax.axis_size("grp")
    index = lax.axis_index("grp")
    block = w_out.shape[1] // size
    kept = [
        jnp.dot(attention, w_out[:, b * block : (b + 1) * block], preferred_element_type=jnp.float32)
        for b in range(size)
    ]
    step = 1
    while step < size:
        high = (index & step) != 0
        keep = [jnp.where(high, kept[k + 1], kept[k]) for k in range(0, len(kept), 2)]
        give = jnp.concatenate(
            [jnp.where(high, kept[k], kept[k + 1]) for k in range(0, len(kept), 2)], axis=1
        )
        if step * 2 == size:
            give = give.astype(jnp.bfloat16)
        moved = lax.ppermute(give, "grp", [(g, g ^ step) for g in range(size)]).astype(jnp.float32)
        kept = [part + moved[:, k * block : (k + 1) * block] for k, part in enumerate(keep)]
        step *= 2
    return kept[0]


def pick(table, index):
    ids = jnp.arange(table.shape[0], dtype=jnp.int32)
    return jnp.sum(jnp.where(ids == index, table, 0))


def shards(
    queries,
    new_keys,
    new_values,
    residual,
    w_out,
    leaf_keys,
    leaf_values,
    upper_keys,
    upper_values,
    req_len,
    leaf_mid,
    mid_root,
    upper_len,
    leaf_len,
):
    dev_count = lax.axis_size("tok")
    my_index = lax.axis_index("tok")
    row_count = queries.shape[0]
    col_count = queries.shape[1]
    head_count = col_count // HEAD_DIM
    mid_count = mid_root.shape[0]
    node_count = upper_len.shape[0]
    root_count = node_count - mid_count
    chunk = upper_keys.shape[1]

    dest_mid = leaf_mid.astype(jnp.int32)
    mid_ids = jnp.arange(mid_count, dtype=jnp.int32)
    dest_root = jnp.sum(
        jnp.where(dest_mid[:, None] == mid_ids[None, :], mid_root[None, :], 0), axis=1
    )
    dest_nodes = jnp.stack([dest_root, root_count + dest_mid], axis=1)
    both = jnp.concatenate([upper_keys, upper_values], axis=0)
    slots = jnp.concatenate([dest_nodes, node_count + dest_nodes], axis=1).T
    send = both.at[slots].get(mode="promise_in_bounds")
    received = lax.all_to_all(send, "tok", 1, 1, tiled=True)
    recv_keys = received[:2]
    recv_values = received[2:]

    my_length = pick(req_len, my_index)
    my_mid = pick(leaf_mid, my_index)
    my_leaf_len = pick(leaf_len, my_index)
    my_root = pick(mid_root, my_mid)
    root_len = pick(upper_len, my_root)
    mid_len = pick(upper_len, root_count + my_mid)
    position = jnp.arange(row_count, dtype=jnp.int32)
    is_live = position < my_length
    leaf_count = leaf_keys.shape[1]
    local_keys = jnp.concatenate([leaf_keys[0], new_keys], axis=0)
    local_values = jnp.concatenate([leaf_values[0], new_values], axis=0)
    leaf_allowed = jnp.broadcast_to(
        (jnp.arange(leaf_count) < my_leaf_len)[None, :], (row_count, leaf_count)
    )
    new_allowed = (position[None, :] <= position[:, None]) & is_live[None, :]
    local_part = partial_attention(
        queries,
        local_keys,
        local_values,
        jnp.concatenate([leaf_allowed, new_allowed], axis=1),
        head_count,
    )

    upper_pos = (
        jnp.arange(dev_count, dtype=jnp.int32)[None, :, None] * chunk
        + jnp.arange(chunk, dtype=jnp.int32)[None, None, :]
    )
    upper_limit = jnp.stack([root_len, mid_len])[:, None, None]
    upper_ok = (upper_pos < upper_limit).reshape(-1)
    upper_part = partial_attention(
        queries,
        recv_keys.reshape(-1, col_count),
        recv_values.reshape(-1, col_count),
        upper_ok[None, :],
        head_count,
    )
    merged = combine(local_part, upper_part)
    attended = jnp.concatenate([part[2] / part[1] for part in merged], axis=1)
    attention = jnp.where(is_live[:, None], attended, 0.0).astype(jnp.bfloat16)
    mixed = project_over_grp(attention, w_out)
    return (residual.astype(jnp.float32) + mixed).astype(jnp.bfloat16)


def solution(mesh):
    in_specs = (
        P("tok", "grp"),
        P("tok", "grp"),
        P("tok", "grp"),
        P("tok", "grp"),
        P("grp", None),
        P("tok", None, "grp"),
        P("tok", None, "grp"),
        P(None, "tok", "grp"),
        P(None, "tok", "grp"),
        P(),
        P(),
        P(),
        P(),
        P(),
    )
    out_specs = P("tok", "grp")
    return jax.shard_map(shards, mesh=mesh, in_specs=in_specs, out_specs=out_specs, check_vma=False)
```

```python
import jax
import jax.numpy as jnp
from jax import lax
from jax.sharding import PartitionSpec as P

HEAD_DIM = 128


NEG_FILL = -1e30


def partial_attention(query_rows, key_rows, values, allowed, head_count):
    head_width = query_rows.shape[1] // head_count
    parts = []
    for head in range(head_count):
        cols = slice(head * head_width, (head + 1) * head_width)
        scores = lax.dot_general(
            query_rows[:, cols],
            key_rows[:, cols],
            (((1,), (1,)), ((), ())),
            preferred_element_type=jnp.float32,
        ) * head_width ** (-0.5)
        scores = jnp.where(allowed, scores, NEG_FILL)
        row_max = jnp.max(scores, axis=1, keepdims=True)
        exp_scores = jnp.where(allowed, jnp.exp(scores - row_max), 0.0)
        row_total = jnp.sum(exp_scores, axis=1, keepdims=True)
        weighted = jnp.dot(
            exp_scores.astype(jnp.bfloat16),
            values[:, cols],
            preferred_element_type=jnp.float32,
        )
        parts.append((row_max, row_total, weighted))
    return parts


def combine(earlier, latter):
    merged = []
    for (max_a, total_a, sum_a), (max_b, total_b, sum_b) in zip(earlier, latter):
        new_max = jnp.maximum(max_a, max_b)
        scale_a = jnp.exp(max_a - new_max)
        scale_b = jnp.exp(max_b - new_max)
        merged.append(
            (new_max, total_a * scale_a + total_b * scale_b, sum_a * scale_a + sum_b * scale_b)
        )
    return merged


def project_over_grp(attention, w_out):
    size = lax.axis_size("grp")
    index = lax.axis_index("grp")
    block = w_out.shape[1] // size
    kept = [
        jnp.dot(attention, w_out[:, b * block : (b + 1) * block], preferred_element_type=jnp.float32)
        for b in range(size)
    ]
    step = 1
    while step < size:
        high = (index & step) != 0
        keep = [jnp.where(high, kept[k + 1], kept[k]) for k in range(0, len(kept), 2)]
        give = jnp.concatenate(
            [jnp.where(high, kept[k], kept[k + 1]) for k in range(0, len(kept), 2)], axis=1
        )
        if step * 2 == size:
            give = give.astype(jnp.bfloat16)
        moved = lax.ppermute(give, "grp", [(g, g ^ step) for g in range(size)]).astype(jnp.float32)
        kept = [part + moved[:, k * block : (k + 1) * block] for k, part in enumerate(keep)]
        step *= 2
    return kept[0]


def pick(table, index):
    ids = jnp.arange(table.shape[0], dtype=jnp.int32)
    return jnp.sum(jnp.where(ids == index, table, 0))


def shards(
    queries,
    new_keys,
    new_values,
    residual,
    w_out,
    leaf_keys,
    leaf_values,
    upper_keys,
    upper_values,
    req_len,
    leaf_mid,
    mid_root,
    upper_len,
    leaf_len,
):
    dev_count = lax.axis_size("tok")
    my_index = lax.axis_index("tok")
    row_count = queries.shape[0]
    col_count = queries.shape[1]
    head_count = col_count // HEAD_DIM
    mid_count = mid_root.shape[0]
    node_count = upper_len.shape[0]
    root_count = node_count - mid_count
    chunk = upper_keys.shape[1]

    dest_mid = leaf_mid.astype(jnp.int32)
    mid_ids = jnp.arange(mid_count, dtype=jnp.int32)
    dest_root = jnp.sum(
        jnp.where(dest_mid[:, None] == mid_ids[None, :], mid_root[None, :], 0), axis=1
    )
    dest_nodes = jnp.stack([dest_root, root_count + dest_mid], axis=1)
    both = jnp.concatenate([upper_keys, upper_values], axis=2)
    send = both.at[dest_nodes].get(mode="promise_in_bounds")
    received = lax.all_to_all(send, "tok", 0, 0, tiled=True).reshape(-1, 2 * col_count)

    my_length = pick(req_len, my_index)
    my_mid = pick(leaf_mid, my_index)
    my_leaf_len = pick(leaf_len, my_index)
    my_root = pick(mid_root, my_mid)
    root_len = pick(upper_len, my_root)
    mid_len = pick(upper_len, root_count + my_mid)
    position = jnp.arange(row_count, dtype=jnp.int32)
    is_live = position < my_length
    leaf_count = leaf_keys.shape[1]
    local_keys = jnp.concatenate([leaf_keys[0], new_keys], axis=0)
    local_values = jnp.concatenate([leaf_values[0], new_values], axis=0)
    leaf_allowed = jnp.broadcast_to(
        (jnp.arange(leaf_count) < my_leaf_len)[None, :], (row_count, leaf_count)
    )
    new_allowed = (position[None, :] <= position[:, None]) & is_live[None, :]
    local_part = partial_attention(
        queries,
        local_keys,
        local_values,
        jnp.concatenate([leaf_allowed, new_allowed], axis=1),
        head_count,
    )

    upper_pos = (
        jnp.arange(dev_count, dtype=jnp.int32)[:, None, None] * chunk
        + jnp.arange(chunk, dtype=jnp.int32)[None, None, :]
    )
    upper_limit = jnp.stack([root_len, mid_len])[None, :, None]
    upper_ok = (upper_pos < upper_limit).reshape(-1)
    upper_part = partial_attention(
        queries,
        received[:, :col_count],
        received[:, col_count:],
        upper_ok[None, :],
        head_count,
    )
    merged = combine(local_part, upper_part)
    attended = jnp.concatenate([part[2] / part[1] for part in merged], axis=1)
    attention = jnp.where(is_live[:, None], attended, 0.0).astype(jnp.bfloat16)
    mixed = project_over_grp(attention, w_out)
    return (residual.astype(jnp.float32) + mixed).astype(jnp.bfloat16)


def solution(mesh):
    in_specs = (
        P("tok", "grp"),
        P("tok", "grp"),
        P("tok", "grp"),
        P("tok", "grp"),
        P("grp", None),
        P("tok", None, "grp"),
        P("tok", None, "grp"),
        P(None, "tok", "grp"),
        P(None, "tok", "grp"),
        P(),
        P(),
        P(),
        P(),
        P(),
    )
    out_specs = P("tok", "grp")
    return jax.shard_map(shards, mesh=mesh, in_specs=in_specs, out_specs=out_specs, check_vma=False)
```

```python
import jax
import jax.numpy as jnp
from jax import lax
from jax.experimental import pallas as pl
from jax.experimental.pallas import tpu as pltpu
from jax.sharding import PartitionSpec as P

HEAD_DIM = 128


NEG_FILL = -1e30


def partial_attention(query_rows, key_rows, values, allowed, head_count):
    head_width = query_rows.shape[1] // head_count
    parts = []
    for head in range(head_count):
        cols = slice(head * head_width, (head + 1) * head_width)
        scores = lax.dot_general(
            query_rows[:, cols],
            key_rows[:, cols],
            (((1,), (1,)), ((), ())),
            preferred_element_type=jnp.float32,
        ) * head_width ** (-0.5)
        scores = jnp.where(allowed, scores, NEG_FILL)
        row_max = jnp.max(scores, axis=1, keepdims=True)
        exp_scores = jnp.where(allowed, jnp.exp(scores - row_max), 0.0)
        row_total = jnp.sum(exp_scores, axis=1, keepdims=True)
        weighted = jnp.dot(
            exp_scores.astype(jnp.bfloat16),
            values[:, cols],
            preferred_element_type=jnp.float32,
        )
        parts.append((row_max, row_total, weighted))
    return parts


def combine(earlier, latter):
    merged = []
    for (max_a, total_a, sum_a), (max_b, total_b, sum_b) in zip(earlier, latter):
        new_max = jnp.maximum(max_a, max_b)
        scale_a = jnp.exp(max_a - new_max)
        scale_b = jnp.exp(max_b - new_max)
        merged.append(
            (new_max, total_a * scale_a + total_b * scale_b, sum_a * scale_a + sum_b * scale_b)
        )
    return merged


def upper_merge(queries, received, local_max, local_total, local_sum, lens, head_width):
    rows, cols = queries.shape
    srcs, _, chunk, _ = received.shape
    heads = cols // head_width
    keys = srcs * 2 * chunk
    scale = head_width ** (-0.5)

    def kernel(lens_ref, q_ref, k_ref, v_ref, m_ref, l_ref, o_ref, out_ref):
        k = k_ref[...].reshape(keys, head_width)
        v = v_ref[...].reshape(keys, head_width)
        s = lax.dot_general(q_ref[...], k, (((1,), (1,)), ((), ())),
                            preferred_element_type=jnp.float32) * scale
        col = lax.broadcasted_iota(jnp.int32, (1, keys), 1)
        src = col // (2 * chunk)
        slot = (col // chunk) % 2
        pos = src * chunk + col % chunk
        allowed = pos < jnp.where(slot == 0, lens_ref[0], lens_ref[1])
        s = jnp.where(allowed, s, NEG_FILL)
        up_max = jnp.max(s, axis=1, keepdims=True)
        p = jnp.where(allowed, jnp.exp(s - up_max), 0.0)
        up_total = jnp.sum(p, axis=1, keepdims=True)
        up_sum = jnp.dot(p.astype(jnp.bfloat16), v, preferred_element_type=jnp.float32)
        lo_max = m_ref[0]
        new_max = jnp.maximum(lo_max, up_max)
        scale_a = jnp.exp(lo_max - new_max)
        scale_b = jnp.exp(up_max - new_max)
        total = l_ref[0] * scale_a + up_total * scale_b
        out_ref[...] = (o_ref[...] * scale_a + up_sum * scale_b) / total

    return pl.pallas_call(
        kernel,
        out_shape=jax.ShapeDtypeStruct((rows, cols), jnp.float32),
        grid_spec=pltpu.PrefetchScalarGridSpec(
            num_scalar_prefetch=1,
            grid=(heads,),
            in_specs=[
                pl.BlockSpec((rows, head_width), lambda h, lens: (0, h)),
                pl.BlockSpec((srcs, 2, chunk, head_width), lambda h, lens: (0, 0, 0, h)),
                pl.BlockSpec((srcs, 2, chunk, head_width), lambda h, lens: (0, 1, 0, h)),
                pl.BlockSpec((1, rows, 1), lambda h, lens: (h, 0, 0)),
                pl.BlockSpec((1, rows, 1), lambda h, lens: (h, 0, 0)),
                pl.BlockSpec((rows, head_width), lambda h, lens: (0, h)),
            ],
            out_specs=pl.BlockSpec((rows, head_width), lambda h, lens: (0, h)),
        ),
    )(lens, queries, received, received, local_max, local_total, local_sum)

def project_over_grp(attention, w_out):
    size = lax.axis_size("grp")
    index = lax.axis_index("grp")
    block = w_out.shape[1] // size
    kept = [
        jnp.dot(attention, w_out[:, b * block : (b + 1) * block], preferred_element_type=jnp.float32)
        for b in range(size)
    ]
    step = 1
    while step < size:
        high = (index & step) != 0
        keep = [jnp.where(high, kept[k + 1], kept[k]) for k in range(0, len(kept), 2)]
        give = jnp.concatenate(
            [jnp.where(high, kept[k], kept[k + 1]) for k in range(0, len(kept), 2)], axis=1
        )
        if step * 2 == size:
            give = give.astype(jnp.bfloat16)
        moved = lax.ppermute(give, "grp", [(g, g ^ step) for g in range(size)]).astype(jnp.float32)
        kept = [part + moved[:, k * block : (k + 1) * block] for k, part in enumerate(keep)]
        step *= 2
    return kept[0]


def pick(table, index):
    ids = jnp.arange(table.shape[0], dtype=jnp.int32)
    return jnp.sum(jnp.where(ids == index, table, 0))


def shards(
    queries,
    new_keys,
    new_values,
    residual,
    w_out,
    leaf_keys,
    leaf_values,
    upper_keys,
    upper_values,
    req_len,
    leaf_mid,
    mid_root,
    upper_len,
    leaf_len,
):
    dev_count = lax.axis_size("tok")
    my_index = lax.axis_index("tok")
    row_count = queries.shape[0]
    col_count = queries.shape[1]
    head_count = col_count // HEAD_DIM
    mid_count = mid_root.shape[0]
    node_count = upper_len.shape[0]
    root_count = node_count - mid_count
    chunk = upper_keys.shape[1]

    dest_mid = leaf_mid.astype(jnp.int32)
    mid_ids = jnp.arange(mid_count, dtype=jnp.int32)
    dest_root = jnp.sum(
        jnp.where(dest_mid[:, None] == mid_ids[None, :], mid_root[None, :], 0), axis=1
    )
    dest_nodes = jnp.stack([dest_root, root_count + dest_mid], axis=1)
    both = jnp.concatenate([upper_keys, upper_values], axis=0)
    send = both.at[jnp.concatenate([dest_nodes, node_count + dest_nodes], axis=1)].get(
        mode="promise_in_bounds"
    )
    received = lax.all_to_all(send, "tok", 0, 0, tiled=True)

    my_length = pick(req_len, my_index)
    my_mid = pick(leaf_mid, my_index)
    my_leaf_len = pick(leaf_len, my_index)
    my_root = pick(mid_root, my_mid)
    root_len = pick(upper_len, my_root)
    mid_len = pick(upper_len, root_count + my_mid)
    position = jnp.arange(row_count, dtype=jnp.int32)
    is_live = position < my_length
    leaf_count = leaf_keys.shape[1]
    local_keys = jnp.concatenate([leaf_keys[0], new_keys], axis=0)
    local_values = jnp.concatenate([leaf_values[0], new_values], axis=0)
    leaf_allowed = jnp.broadcast_to(
        (jnp.arange(leaf_count) < my_leaf_len)[None, :], (row_count, leaf_count)
    )
    new_allowed = (position[None, :] <= position[:, None]) & is_live[None, :]
    local_part = partial_attention(
        queries,
        local_keys,
        local_values,
        jnp.concatenate([leaf_allowed, new_allowed], axis=1),
        head_count,
    )

    attended = upper_merge(
        queries,
        received,
        jnp.stack([part[0] for part in local_part]),
        jnp.stack([part[1] for part in local_part]),
        jnp.concatenate([part[2] for part in local_part], axis=1),
        jnp.stack([root_len, mid_len]).astype(jnp.int32),
        col_count // head_count,
    )
    attention = jnp.where(is_live[:, None], attended, 0.0).astype(jnp.bfloat16)
    mixed = project_over_grp(attention, w_out)
    return (residual.astype(jnp.float32) + mixed).astype(jnp.bfloat16)


def solution(mesh):
    in_specs = (
        P("tok", "grp"),
        P("tok", "grp"),
        P("tok", "grp"),
        P("tok", "grp"),
        P("grp", None),
        P("tok", None, "grp"),
        P("tok", None, "grp"),
        P(None, "tok", "grp"),
        P(None, "tok", "grp"),
        P(),
        P(),
        P(),
        P(),
        P(),
    )
    out_specs = P("tok", "grp")
    return jax.shard_map(shards, mesh=mesh, in_specs=in_specs, out_specs=out_specs, check_vma=False)
```

```python
import jax
import jax.numpy as jnp
from jax import lax
from jax.experimental import pallas as pl
from jax.experimental.pallas import tpu as pltpu
from jax.sharding import PartitionSpec as P

HEAD_DIM = 128


NEG_FILL = -1e30


def partial_attention(query_rows, key_rows, values, allowed, head_count):
    head_width = query_rows.shape[1] // head_count
    parts = []
    for head in range(head_count):
        cols = slice(head * head_width, (head + 1) * head_width)
        scores = lax.dot_general(
            query_rows[:, cols],
            key_rows[:, cols],
            (((1,), (1,)), ((), ())),
            preferred_element_type=jnp.float32,
        ) * head_width ** (-0.5)
        scores = jnp.where(allowed, scores, NEG_FILL)
        row_max = jnp.max(scores, axis=1, keepdims=True)
        exp_scores = jnp.where(allowed, jnp.exp(scores - row_max), 0.0)
        row_total = jnp.sum(exp_scores, axis=1, keepdims=True)
        weighted = jnp.dot(
            exp_scores.astype(jnp.bfloat16),
            values[:, cols],
            preferred_element_type=jnp.float32,
        )
        parts.append((row_max, row_total, weighted))
    return parts


def combine(earlier, latter):
    merged = []
    for (max_a, total_a, sum_a), (max_b, total_b, sum_b) in zip(earlier, latter):
        new_max = jnp.maximum(max_a, max_b)
        scale_a = jnp.exp(max_a - new_max)
        scale_b = jnp.exp(max_b - new_max)
        merged.append(
            (new_max, total_a * scale_a + total_b * scale_b, sum_a * scale_a + sum_b * scale_b)
        )
    return merged


def upper_merge(queries, received, local_max, local_total, local_sum, lens, head_width):
    rows, cols = queries.shape
    srcs, _, chunk, _ = received.shape
    heads = cols // head_width
    keys = srcs * 2 * chunk
    scale = head_width ** (-0.5)

    def kernel(lens_ref, q_ref, r_ref, m_ref, l_ref, o_ref, out_ref):
        col = lax.broadcasted_iota(jnp.int32, (1, keys), 1)
        src = col // (2 * chunk)
        slot = (col // chunk) % 2
        pos = src * chunk + col % chunk
        allowed = pos < jnp.where(slot == 0, lens_ref[0], lens_ref[1])
        for head in range(heads):
            cols_h = slice(head * head_width, (head + 1) * head_width)
            k = r_ref[:, 0:2, :, cols_h].reshape(keys, head_width)
            v = r_ref[:, 2:4, :, cols_h].reshape(keys, head_width)
            s = lax.dot_general(q_ref[:, cols_h], k, (((1,), (1,)), ((), ())),
                                preferred_element_type=jnp.float32) * scale
            s = jnp.where(allowed, s, NEG_FILL)
            up_max = jnp.max(s, axis=1, keepdims=True)
            p = jnp.where(allowed, jnp.exp(s - up_max), 0.0)
            up_total = jnp.sum(p, axis=1, keepdims=True)
            up_sum = jnp.dot(p.astype(jnp.bfloat16), v, preferred_element_type=jnp.float32)
            lo_max = m_ref[head]
            new_max = jnp.maximum(lo_max, up_max)
            scale_a = jnp.exp(lo_max - new_max)
            scale_b = jnp.exp(up_max - new_max)
            total = l_ref[head] * scale_a + up_total * scale_b
            out_ref[:, cols_h] = (o_ref[:, cols_h] * scale_a + up_sum * scale_b) / total

    return pl.pallas_call(
        kernel,
        out_shape=jax.ShapeDtypeStruct((rows, cols), jnp.float32),
        grid_spec=pltpu.PrefetchScalarGridSpec(
            num_scalar_prefetch=1,
            grid=(1,),
            in_specs=[
                pl.BlockSpec((rows, cols), lambda i, lens: (0, 0)),
                pl.BlockSpec(received.shape, lambda i, lens: (0, 0, 0, 0)),
                pl.BlockSpec(local_max.shape, lambda i, lens: (0, 0, 0)),
                pl.BlockSpec(local_total.shape, lambda i, lens: (0, 0, 0)),
                pl.BlockSpec((rows, cols), lambda i, lens: (0, 0)),
            ],
            out_specs=pl.BlockSpec((rows, cols), lambda i, lens: (0, 0)),
        ),
    )(lens, queries, received, local_max, local_total, local_sum)


def project_over_grp(attention, w_out):
    size = lax.axis_size("grp")
    index = lax.axis_index("grp")
    block = w_out.shape[1] // size
    kept = [
        jnp.dot(attention, w_out[:, b * block : (b + 1) * block], preferred_element_type=jnp.float32)
        for b in range(size)
    ]
    step = 1
    while step < size:
        high = (index & step) != 0
        keep = [jnp.where(high, kept[k + 1], kept[k]) for k in range(0, len(kept), 2)]
        give = jnp.concatenate(
            [jnp.where(high, kept[k], kept[k + 1]) for k in range(0, len(kept), 2)], axis=1
        )
        if step * 2 == size:
            give = give.astype(jnp.bfloat16)
        moved = lax.ppermute(give, "grp", [(g, g ^ step) for g in range(size)]).astype(jnp.float32)
        kept = [part + moved[:, k * block : (k + 1) * block] for k, part in enumerate(keep)]
        step *= 2
    return kept[0]


def pick(table, index):
    ids = jnp.arange(table.shape[0], dtype=jnp.int32)
    return jnp.sum(jnp.where(ids == index, table, 0))


def shards(
    queries,
    new_keys,
    new_values,
    residual,
    w_out,
    leaf_keys,
    leaf_values,
    upper_keys,
    upper_values,
    req_len,
    leaf_mid,
    mid_root,
    upper_len,
    leaf_len,
):
    dev_count = lax.axis_size("tok")
    my_index = lax.axis_index("tok")
    row_count = queries.shape[0]
    col_count = queries.shape[1]
    head_count = col_count // HEAD_DIM
    mid_count = mid_root.shape[0]
    node_count = upper_len.shape[0]
    root_count = node_count - mid_count
    chunk = upper_keys.shape[1]

    dest_mid = leaf_mid.astype(jnp.int32)
    mid_ids = jnp.arange(mid_count, dtype=jnp.int32)
    dest_root = jnp.sum(
        jnp.where(dest_mid[:, None] == mid_ids[None, :], mid_root[None, :], 0), axis=1
    )
    dest_nodes = jnp.stack([dest_root, root_count + dest_mid], axis=1)
    both = jnp.concatenate([upper_keys, upper_values], axis=0)
    send = both.at[jnp.concatenate([dest_nodes, node_count + dest_nodes], axis=1)].get(
        mode="promise_in_bounds"
    )
    received = lax.all_to_all(send, "tok", 0, 0, tiled=True)

    my_length = pick(req_len, my_index)
    my_mid = pick(leaf_mid, my_index)
    my_leaf_len = pick(leaf_len, my_index)
    my_root = pick(mid_root, my_mid)
    root_len = pick(upper_len, my_root)
    mid_len = pick(upper_len, root_count + my_mid)
    position = jnp.arange(row_count, dtype=jnp.int32)
    is_live = position < my_length
    leaf_count = leaf_keys.shape[1]
    local_keys = jnp.concatenate([leaf_keys[0], new_keys], axis=0)
    local_values = jnp.concatenate([leaf_values[0], new_values], axis=0)
    leaf_allowed = jnp.broadcast_to(
        (jnp.arange(leaf_count) < my_leaf_len)[None, :], (row_count, leaf_count)
    )
    new_allowed = (position[None, :] <= position[:, None]) & is_live[None, :]
    local_part = partial_attention(
        queries,
        local_keys,
        local_values,
        jnp.concatenate([leaf_allowed, new_allowed], axis=1),
        head_count,
    )

    attended = upper_merge(
        queries,
        received,
        jnp.stack([part[0] for part in local_part]),
        jnp.stack([part[1] for part in local_part]),
        jnp.concatenate([part[2] for part in local_part], axis=1),
        jnp.stack([root_len, mid_len]).astype(jnp.int32),
        col_count // head_count,
    )
    attention = jnp.where(is_live[:, None], attended, 0.0).astype(jnp.bfloat16)
    mixed = project_over_grp(attention, w_out)
    return (residual.astype(jnp.float32) + mixed).astype(jnp.bfloat16)


def solution(mesh):
    in_specs = (
        P("tok", "grp"),
        P("tok", "grp"),
        P("tok", "grp"),
        P("tok", "grp"),
        P("grp", None),
        P("tok", None, "grp"),
        P("tok", None, "grp"),
        P(None, "tok", "grp"),
        P(None, "tok", "grp"),
        P(),
        P(),
        P(),
        P(),
        P(),
    )
    out_specs = P("tok", "grp")
    return jax.shard_map(shards, mesh=mesh, in_specs=in_specs, out_specs=out_specs, check_vma=False)
```

```python
import jax
import jax.numpy as jnp
from jax import lax
from jax.sharding import PartitionSpec as P

HEAD_DIM = 128


NEG_FILL = -1e30


def partial_attention(query_rows, key_rows, values, allowed, head_count):
    head_width = query_rows.shape[1] // head_count
    parts = []
    for head in range(head_count):
        cols = slice(head * head_width, (head + 1) * head_width)
        scores = lax.dot_general(
            query_rows[:, cols],
            key_rows[:, cols],
            (((1,), (1,)), ((), ())),
            preferred_element_type=jnp.float32,
        ) * head_width ** (-0.5)
        scores = jnp.where(allowed, scores, NEG_FILL)
        row_max = jnp.max(scores, axis=1, keepdims=True)
        exp_scores = jnp.where(allowed, jnp.exp(scores - row_max), 0.0)
        row_total = jnp.sum(exp_scores, axis=1, keepdims=True)
        weighted = jnp.dot(
            exp_scores.astype(jnp.bfloat16),
            values[:, cols],
            preferred_element_type=jnp.float32,
        )
        parts.append((row_max, row_total, weighted))
    return parts


def combine(earlier, latter):
    merged = []
    for (max_a, total_a, sum_a), (max_b, total_b, sum_b) in zip(earlier, latter):
        new_max = jnp.maximum(max_a, max_b)
        scale_a = jnp.exp(max_a - new_max)
        scale_b = jnp.exp(max_b - new_max)
        merged.append(
            (new_max, total_a * scale_a + total_b * scale_b, sum_a * scale_a + sum_b * scale_b)
        )
    return merged


def project_over_grp(attention, w_out):
    size = lax.axis_size("grp")
    index = lax.axis_index("grp")
    block = w_out.shape[1] // size
    kept = [
        jnp.dot(attention, w_out[:, b * block : (b + 1) * block], preferred_element_type=jnp.float32)
        for b in range(size)
    ]
    step = 1
    while step < size:
        high = (index & step) != 0
        keep = [jnp.where(high, kept[k + 1], kept[k]) for k in range(0, len(kept), 2)]
        give = jnp.concatenate(
            [jnp.where(high, kept[k], kept[k + 1]) for k in range(0, len(kept), 2)], axis=1
        )
        give = give.astype(jnp.bfloat16)
        moved = lax.ppermute(give, "grp", [(g, g ^ step) for g in range(size)]).astype(jnp.float32)
        kept = [part + moved[:, k * block : (k + 1) * block] for k, part in enumerate(keep)]
        step *= 2
    return kept[0]


def pick(table, index):
    ids = jnp.arange(table.shape[0], dtype=jnp.int32)
    return jnp.sum(jnp.where(ids == index, table, 0))


def shards(
    queries,
    new_keys,
    new_values,
    residual,
    w_out,
    leaf_keys,
    leaf_values,
    upper_keys,
    upper_values,
    req_len,
    leaf_mid,
    mid_root,
    upper_len,
    leaf_len,
):
    dev_count = lax.axis_size("tok")
    my_index = lax.axis_index("tok")
    row_count = queries.shape[0]
    col_count = queries.shape[1]
    head_count = col_count // HEAD_DIM
    mid_count = mid_root.shape[0]
    node_count = upper_len.shape[0]
    root_count = node_count - mid_count
    chunk = upper_keys.shape[1]

    dest_mid = leaf_mid.astype(jnp.int32)
    mid_ids = jnp.arange(mid_count, dtype=jnp.int32)
    dest_root = jnp.sum(
        jnp.where(dest_mid[:, None] == mid_ids[None, :], mid_root[None, :], 0), axis=1
    )
    dest_nodes = jnp.stack([dest_root, root_count + dest_mid], axis=1)
    both = jnp.concatenate([upper_keys, upper_values], axis=0)
    send = both.at[jnp.concatenate([dest_nodes, node_count + dest_nodes], axis=1)].get(
        mode="promise_in_bounds"
    )
    received = lax.all_to_all(send, "tok", 0, 0, tiled=True)
    recv_keys = received[:, :2]
    recv_values = received[:, 2:]

    my_length = pick(req_len, my_index)
    my_mid = pick(leaf_mid, my_index)
    my_leaf_len = pick(leaf_len, my_index)
    my_root = pick(mid_root, my_mid)
    root_len = pick(upper_len, my_root)
    mid_len = pick(upper_len, root_count + my_mid)
    position = jnp.arange(row_count, dtype=jnp.int32)
    is_live = position < my_length
    leaf_count = leaf_keys.shape[1]
    local_keys = jnp.concatenate([leaf_keys[0], new_keys], axis=0)
    local_values = jnp.concatenate([leaf_values[0], new_values], axis=0)
    leaf_allowed = jnp.broadcast_to(
        (jnp.arange(leaf_count) < my_leaf_len)[None, :], (row_count, leaf_count)
    )
    new_allowed = (position[None, :] <= position[:, None]) & is_live[None, :]
    local_part = partial_attention(
        queries,
        local_keys,
        local_values,
        jnp.concatenate([leaf_allowed, new_allowed], axis=1),
        head_count,
    )

    upper_pos = (
        jnp.arange(dev_count, dtype=jnp.int32)[:, None, None] * chunk
        + jnp.arange(chunk, dtype=jnp.int32)[None, None, :]
    )
    upper_limit = jnp.stack([root_len, mid_len])[None, :, None]
    upper_ok = (upper_pos < upper_limit).reshape(-1)
    upper_part = partial_attention(
        queries,
        recv_keys.reshape(-1, col_count),
        recv_values.reshape(-1, col_count),
        upper_ok[None, :],
        head_count,
    )
    merged = combine(local_part, upper_part)
    attended = jnp.concatenate([part[2] / part[1] for part in merged], axis=1)
    attention = jnp.where(is_live[:, None], attended, 0.0).astype(jnp.bfloat16)
    mixed = project_over_grp(attention, w_out)
    return (residual.astype(jnp.float32) + mixed).astype(jnp.bfloat16)


def solution(mesh):
    in_specs = (
        P("tok", "grp"),
        P("tok", "grp"),
        P("tok", "grp"),
        P("tok", "grp"),
        P("grp", None),
        P("tok", None, "grp"),
        P("tok", None, "grp"),
        P(None, "tok", "grp"),
        P(None, "tok", "grp"),
        P(),
        P(),
        P(),
        P(),
        P(),
    )
    out_specs = P("tok", "grp")
    return jax.shard_map(shards, mesh=mesh, in_specs=in_specs, out_specs=out_specs, check_vma=False)
```

```python
import jax
import jax.numpy as jnp
from jax import lax
from jax.sharding import PartitionSpec as P

HEAD_DIM = 128


NEG_FILL = -1e30


def partial_attention(query_rows, key_rows, values, allowed, head_count):
    head_width = query_rows.shape[1] // head_count
    parts = []
    for head in range(head_count):
        cols = slice(head * head_width, (head + 1) * head_width)
        scores = lax.dot_general(
            query_rows[:, cols],
            key_rows[:, cols],
            (((1,), (1,)), ((), ())),
            preferred_element_type=jnp.float32,
        ) * head_width ** (-0.5)
        scores = jnp.where(allowed, scores, NEG_FILL)
        row_max = jnp.max(scores, axis=1, keepdims=True)
        exp_scores = jnp.where(allowed, jnp.exp(scores - row_max), 0.0)
        row_total = jnp.sum(exp_scores, axis=1, keepdims=True)
        weighted = jnp.dot(
            exp_scores.astype(jnp.bfloat16),
            values[:, cols],
            preferred_element_type=jnp.float32,
        )
        parts.append((row_max, row_total, weighted))
    return parts


def combine(earlier, latter):
    merged = []
    for (max_a, total_a, sum_a), (max_b, total_b, sum_b) in zip(earlier, latter):
        new_max = jnp.maximum(max_a, max_b)
        scale_a = jnp.exp(max_a - new_max)
        scale_b = jnp.exp(max_b - new_max)
        merged.append(
            (new_max, total_a * scale_a + total_b * scale_b, sum_a * scale_a + sum_b * scale_b)
        )
    return merged


def project_over_grp(attention, w_blocks, residual):
    size = lax.axis_size("grp")
    index = lax.axis_index("grp")
    block = w_blocks[0].shape[1]
    kept = [jnp.dot(attention, w, preferred_element_type=jnp.float32) for w in w_blocks]
    step = 1
    while step < size:
        high = (index & step) != 0
        keep = [jnp.where(high, kept[k + 1], kept[k]) for k in range(0, len(kept), 2)]
        give = jnp.concatenate(
            [jnp.where(high, kept[k], kept[k + 1]) for k in range(0, len(kept), 2)], axis=1
        )
        give = give.astype(jnp.bfloat16)
        moved = lax.ppermute(give, "grp", [(g, g ^ step) for g in range(size)]).astype(jnp.float32)
        if step * 2 == size:
            keep = [part + residual.astype(jnp.float32) for part in keep]
        kept = [part + moved[:, k * block : (k + 1) * block] for k, part in enumerate(keep)]
        step *= 2
    return kept[0]


def pick(table, index):
    ids = jnp.arange(table.shape[0], dtype=jnp.int32)
    return jnp.sum(jnp.where(ids == index, table, 0))


def shards(
    queries,
    new_keys,
    new_values,
    residual,
    w_out,
    leaf_keys,
    leaf_values,
    upper_keys,
    upper_values,
    req_len,
    leaf_mid,
    mid_root,
    upper_len,
    leaf_len,
):
    dev_count = lax.axis_size("tok")
    my_index = lax.axis_index("tok")
    row_count = queries.shape[0]
    col_count = queries.shape[1]
    head_count = col_count // HEAD_DIM
    mid_count = mid_root.shape[0]
    node_count = upper_len.shape[0]
    root_count = node_count - mid_count
    chunk = upper_keys.shape[1]

    dest_mid = leaf_mid.astype(jnp.int32)
    mid_ids = jnp.arange(mid_count, dtype=jnp.int32)
    dest_root = jnp.sum(
        jnp.where(dest_mid[:, None] == mid_ids[None, :], mid_root[None, :], 0), axis=1
    )
    dest_nodes = jnp.stack([dest_root, root_count + dest_mid], axis=1)
    both = jnp.concatenate([upper_keys, upper_values], axis=0)
    send = both.at[jnp.concatenate([dest_nodes, node_count + dest_nodes], axis=1)].get(
        mode="promise_in_bounds"
    )
    received = lax.all_to_all(send, "tok", 0, 0, tiled=True)
    recv_keys = received[:, :2]
    recv_values = received[:, 2:]

    my_length = pick(req_len, my_index)
    my_mid = pick(leaf_mid, my_index)
    my_leaf_len = pick(leaf_len, my_index)
    my_root = pick(mid_root, my_mid)
    root_len = pick(upper_len, my_root)
    mid_len = pick(upper_len, root_count + my_mid)
    position = jnp.arange(row_count, dtype=jnp.int32)
    is_live = position < my_length
    leaf_count = leaf_keys.shape[1]
    local_keys = jnp.concatenate([leaf_keys[0], new_keys], axis=0)
    local_values = jnp.concatenate([leaf_values[0], new_values], axis=0)
    leaf_allowed = jnp.broadcast_to(
        (jnp.arange(leaf_count) < my_leaf_len)[None, :], (row_count, leaf_count)
    )
    new_allowed = (position[None, :] <= position[:, None]) & is_live[None, :]
    local_part = partial_attention(
        queries,
        local_keys,
        local_values,
        jnp.concatenate([leaf_allowed, new_allowed], axis=1),
        head_count,
    )
    grp_size = lax.axis_size("grp")
    block = w_out.shape[1] // grp_size
    w_blocks = [w_out[:, b * block : (b + 1) * block] for b in range(grp_size)]
    w_blocks, local_part = lax.optimization_barrier((w_blocks, local_part))

    upper_pos = (
        jnp.arange(dev_count, dtype=jnp.int32)[:, None, None] * chunk
        + jnp.arange(chunk, dtype=jnp.int32)[None, None, :]
    )
    upper_limit = jnp.stack([root_len, mid_len])[None, :, None]
    upper_ok = (upper_pos < upper_limit).reshape(-1)
    upper_part = partial_attention(
        queries,
        recv_keys.reshape(-1, col_count),
        recv_values.reshape(-1, col_count),
        upper_ok[None, :],
        head_count,
    )
    merged = combine(local_part, upper_part)
    attended = jnp.concatenate([part[2] / part[1] for part in merged], axis=1)
    attention = jnp.where(is_live[:, None], attended, 0.0).astype(jnp.bfloat16)
    return project_over_grp(attention, w_blocks, residual).astype(jnp.bfloat16)


def solution(mesh):
    in_specs = (
        P("tok", "grp"),
        P("tok", "grp"),
        P("tok", "grp"),
        P("tok", "grp"),
        P("grp", None),
        P("tok", None, "grp"),
        P("tok", None, "grp"),
        P(None, "tok", "grp"),
        P(None, "tok", "grp"),
        P(),
        P(),
        P(),
        P(),
        P(),
    )
    out_specs = P("tok", "grp")
    return jax.shard_map(shards, mesh=mesh, in_specs=in_specs, out_specs=out_specs, check_vma=False)
```

```python
import jax
import jax.numpy as jnp
from jax import lax
from jax.sharding import PartitionSpec as P

HEAD_DIM = 128


NEG_FILL = -1e30


def partial_attention(query_rows, key_rows, values, allowed, head_count):
    head_width = query_rows.shape[1] // head_count
    parts = []
    for head in range(head_count):
        cols = slice(head * head_width, (head + 1) * head_width)
        scores = lax.dot_general(
            query_rows[:, cols],
            key_rows[:, cols],
            (((1,), (1,)), ((), ())),
            preferred_element_type=jnp.float32,
        ) * head_width ** (-0.5)
        scores = jnp.where(allowed, scores, NEG_FILL)
        row_max = jnp.max(scores, axis=1, keepdims=True)
        exp_scores = jnp.where(allowed, jnp.exp(scores - row_max), 0.0)
        row_total = jnp.sum(exp_scores, axis=1, keepdims=True)
        weighted = jnp.dot(
            exp_scores.astype(jnp.bfloat16),
            values[:, cols],
            preferred_element_type=jnp.float32,
        )
        parts.append((row_max, row_total, weighted))
    return parts


def head_attention(query_rows, key_heads, value_heads, allowed):
    head_width = key_heads[0].shape[1]
    parts = []
    for head, (keys, values) in enumerate(zip(key_heads, value_heads)):
        scores = lax.dot_general(
            query_rows[:, head * head_width : (head + 1) * head_width],
            keys,
            (((1,), (1,)), ((), ())),
            preferred_element_type=jnp.float32,
        ) * head_width ** (-0.5)
        scores = jnp.where(allowed, scores, NEG_FILL)
        row_max = jnp.max(scores, axis=1, keepdims=True)
        exp_scores = jnp.where(allowed, jnp.exp(scores - row_max), 0.0)
        row_total = jnp.sum(exp_scores, axis=1, keepdims=True)
        weighted = jnp.dot(
            exp_scores.astype(jnp.bfloat16), values, preferred_element_type=jnp.float32
        )
        parts.append((row_max, row_total, weighted))
    return parts


def combine(earlier, latter):
    merged = []
    for (max_a, total_a, sum_a), (max_b, total_b, sum_b) in zip(earlier, latter):
        new_max = jnp.maximum(max_a, max_b)
        scale_a = jnp.exp(max_a - new_max)
        scale_b = jnp.exp(max_b - new_max)
        merged.append(
            (new_max, total_a * scale_a + total_b * scale_b, sum_a * scale_a + sum_b * scale_b)
        )
    return merged


def project_over_grp(attention, w_blocks, residual):
    size = lax.axis_size("grp")
    index = lax.axis_index("grp")
    block = w_blocks[0].shape[1]
    kept = [jnp.dot(attention, w, preferred_element_type=jnp.float32) for w in w_blocks]
    step = 1
    while step < size:
        high = (index & step) != 0
        keep = [jnp.where(high, kept[k + 1], kept[k]) for k in range(0, len(kept), 2)]
        give = jnp.concatenate(
            [jnp.where(high, kept[k], kept[k + 1]) for k in range(0, len(kept), 2)], axis=1
        )
        give = give.astype(jnp.bfloat16)
        moved = lax.ppermute(give, "grp", [(g, g ^ step) for g in range(size)]).astype(jnp.float32)
        if step * 2 == size:
            keep = [part + residual.astype(jnp.float32) for part in keep]
        kept = [part + moved[:, k * block : (k + 1) * block] for k, part in enumerate(keep)]
        step *= 2
    return kept[0]


def pick(table, index):
    ids = jnp.arange(table.shape[0], dtype=jnp.int32)
    return jnp.sum(jnp.where(ids == index, table, 0))


def shards(
    queries,
    new_keys,
    new_values,
    residual,
    w_out,
    leaf_keys,
    leaf_values,
    upper_keys,
    upper_values,
    req_len,
    leaf_mid,
    mid_root,
    upper_len,
    leaf_len,
):
    dev_count = lax.axis_size("tok")
    my_index = lax.axis_index("tok")
    row_count = queries.shape[0]
    col_count = queries.shape[1]
    head_count = col_count // HEAD_DIM
    mid_count = mid_root.shape[0]
    node_count = upper_len.shape[0]
    root_count = node_count - mid_count
    chunk = upper_keys.shape[1]

    dest_mid = leaf_mid.astype(jnp.int32)
    mid_ids = jnp.arange(mid_count, dtype=jnp.int32)
    dest_root = jnp.sum(
        jnp.where(dest_mid[:, None] == mid_ids[None, :], mid_root[None, :], 0), axis=1
    )
    dest_nodes = jnp.stack([dest_root, root_count + dest_mid], axis=1)
    head_width = col_count // head_count
    both = jnp.concatenate([upper_keys, upper_values], axis=0)
    both = both.reshape(2 * node_count, chunk, head_count, head_width).transpose(0, 2, 1, 3)
    send = both.at[jnp.concatenate([dest_nodes, node_count + dest_nodes], axis=1)].get(
        mode="promise_in_bounds"
    )
    received = lax.all_to_all(send, "tok", 0, 0, tiled=True)

    my_length = pick(req_len, my_index)
    my_mid = pick(leaf_mid, my_index)
    my_leaf_len = pick(leaf_len, my_index)
    my_root = pick(mid_root, my_mid)
    root_len = pick(upper_len, my_root)
    mid_len = pick(upper_len, root_count + my_mid)
    position = jnp.arange(row_count, dtype=jnp.int32)
    is_live = position < my_length
    leaf_count = leaf_keys.shape[1]
    local_keys = jnp.concatenate([leaf_keys[0], new_keys], axis=0)
    local_values = jnp.concatenate([leaf_values[0], new_values], axis=0)
    leaf_allowed = jnp.broadcast_to(
        (jnp.arange(leaf_count) < my_leaf_len)[None, :], (row_count, leaf_count)
    )
    new_allowed = (position[None, :] <= position[:, None]) & is_live[None, :]
    local_part = partial_attention(
        queries,
        local_keys,
        local_values,
        jnp.concatenate([leaf_allowed, new_allowed], axis=1),
        head_count,
    )
    grp_size = lax.axis_size("grp")
    block = w_out.shape[1] // grp_size
    w_blocks = [w_out[:, b * block : (b + 1) * block] for b in range(grp_size)]
    w_blocks, local_part = lax.optimization_barrier((w_blocks, local_part))

    upper_pos = (
        jnp.arange(dev_count, dtype=jnp.int32)[:, None, None] * chunk
        + jnp.arange(chunk, dtype=jnp.int32)[None, None, :]
    )
    upper_limit = jnp.stack([root_len, mid_len])[None, :, None]
    upper_ok = (upper_pos < upper_limit).reshape(-1)
    upper_part = head_attention(
        queries,
        [received[:, :2, head].reshape(-1, head_width) for head in range(head_count)],
        [received[:, 2:, head].reshape(-1, head_width) for head in range(head_count)],
        upper_ok[None, :],
    )
    merged = combine(local_part, upper_part)
    attended = jnp.concatenate([part[2] / part[1] for part in merged], axis=1)
    attention = jnp.where(is_live[:, None], attended, 0.0).astype(jnp.bfloat16)
    return project_over_grp(attention, w_blocks, residual).astype(jnp.bfloat16)


def solution(mesh):
    in_specs = (
        P("tok", "grp"),
        P("tok", "grp"),
        P("tok", "grp"),
        P("tok", "grp"),
        P("grp", None),
        P("tok", None, "grp"),
        P("tok", None, "grp"),
        P(None, "tok", "grp"),
        P(None, "tok", "grp"),
        P(),
        P(),
        P(),
        P(),
        P(),
    )
    out_specs = P("tok", "grp")
    return jax.shard_map(shards, mesh=mesh, in_specs=in_specs, out_specs=out_specs, check_vma=False)
```

```python
import jax
import jax.numpy as jnp
from jax import lax
from jax.sharding import PartitionSpec as P

HEAD_DIM = 128


NEG_FILL = -1e30


def partial_attention(query_rows, key_rows, values, allowed, head_count):
    head_width = query_rows.shape[1] // head_count
    parts = []
    for head in range(head_count):
        cols = slice(head * head_width, (head + 1) * head_width)
        scores = lax.dot_general(
            query_rows[:, cols],
            key_rows[:, cols],
            (((1,), (1,)), ((), ())),
            preferred_element_type=jnp.float32,
        ) * head_width ** (-0.5)
        scores = jnp.where(allowed, scores, NEG_FILL)
        row_max = jnp.max(scores, axis=1, keepdims=True)
        exp_scores = jnp.where(allowed, jnp.exp(scores - row_max), 0.0)
        row_total = jnp.sum(exp_scores, axis=1, keepdims=True)
        weighted = jnp.dot(
            exp_scores.astype(jnp.bfloat16),
            values[:, cols],
            preferred_element_type=jnp.float32,
        )
        parts.append((row_max, row_total, weighted))
    return parts


def combine(earlier, latter):
    merged = []
    for (max_a, total_a, sum_a), (max_b, total_b, sum_b) in zip(earlier, latter):
        new_max = jnp.maximum(max_a, max_b)
        scale_a = jnp.exp(max_a - new_max)
        scale_b = jnp.exp(max_b - new_max)
        merged.append(
            (new_max, total_a * scale_a + total_b * scale_b, sum_a * scale_a + sum_b * scale_b)
        )
    return merged


def project_over_grp(attention, w_blocks, residual):
    size = lax.axis_size("grp")
    index = lax.axis_index("grp")
    block = w_blocks[0].shape[1]
    kept = [jnp.dot(attention, w, preferred_element_type=jnp.float32) for w in w_blocks]
    step = 1
    while step < size:
        high = (index & step) != 0
        keep = [jnp.where(high, kept[k + 1], kept[k]) for k in range(0, len(kept), 2)]
        give = jnp.concatenate(
            [jnp.where(high, kept[k], kept[k + 1]) for k in range(0, len(kept), 2)], axis=1
        )
        give = give.astype(jnp.bfloat16)
        pairs = [(g, g ^ step) for g in range(size)]
        if step * 2 == size:
            half = give.shape[0] // 2
            moved = jnp.concatenate(
                [lax.ppermute(give[:half], "grp", pairs), lax.ppermute(give[half:], "grp", pairs)],
                axis=0,
            ).astype(jnp.float32)
        else:
            moved = lax.ppermute(give, "grp", pairs).astype(jnp.float32)
        if step * 2 == size:
            keep = [part + residual.astype(jnp.float32) for part in keep]
        kept = [part + moved[:, k * block : (k + 1) * block] for k, part in enumerate(keep)]
        step *= 2
    return kept[0]


def pick(table, index):
    ids = jnp.arange(table.shape[0], dtype=jnp.int32)
    return jnp.sum(jnp.where(ids == index, table, 0))


def shards(
    queries,
    new_keys,
    new_values,
    residual,
    w_out,
    leaf_keys,
    leaf_values,
    upper_keys,
    upper_values,
    req_len,
    leaf_mid,
    mid_root,
    upper_len,
    leaf_len,
):
    dev_count = lax.axis_size("tok")
    my_index = lax.axis_index("tok")
    row_count = queries.shape[0]
    col_count = queries.shape[1]
    head_count = col_count // HEAD_DIM
    mid_count = mid_root.shape[0]
    node_count = upper_len.shape[0]
    root_count = node_count - mid_count
    chunk = upper_keys.shape[1]

    dest_mid = leaf_mid.astype(jnp.int32)
    mid_ids = jnp.arange(mid_count, dtype=jnp.int32)
    dest_root = jnp.sum(
        jnp.where(dest_mid[:, None] == mid_ids[None, :], mid_root[None, :], 0), axis=1
    )
    dest_nodes = jnp.stack([dest_root, root_count + dest_mid], axis=1)
    both = jnp.concatenate([upper_keys, upper_values], axis=0)
    send = both.at[jnp.concatenate([dest_nodes, node_count + dest_nodes], axis=1)].get(
        mode="promise_in_bounds"
    )
    received = lax.all_to_all(send, "tok", 0, 0, tiled=True)
    recv_keys = received[:, :2]
    recv_values = received[:, 2:]

    my_length = pick(req_len, my_index)
    my_mid = pick(leaf_mid, my_index)
    my_leaf_len = pick(leaf_len, my_index)
    my_root = pick(mid_root, my_mid)
    root_len = pick(upper_len, my_root)
    mid_len = pick(upper_len, root_count + my_mid)
    position = jnp.arange(row_count, dtype=jnp.int32)
    is_live = position < my_length
    leaf_count = leaf_keys.shape[1]
    local_keys = jnp.concatenate([leaf_keys[0], new_keys], axis=0)
    local_values = jnp.concatenate([leaf_values[0], new_values], axis=0)
    leaf_allowed = jnp.broadcast_to(
        (jnp.arange(leaf_count) < my_leaf_len)[None, :], (row_count, leaf_count)
    )
    new_allowed = (position[None, :] <= position[:, None]) & is_live[None, :]
    local_part = partial_attention(
        queries,
        local_keys,
        local_values,
        jnp.concatenate([leaf_allowed, new_allowed], axis=1),
        head_count,
    )
    grp_size = lax.axis_size("grp")
    block = w_out.shape[1] // grp_size
    w_blocks = [w_out[:, b * block : (b + 1) * block] for b in range(grp_size)]
    w_blocks, local_part = lax.optimization_barrier((w_blocks, local_part))

    upper_pos = (
        jnp.arange(dev_count, dtype=jnp.int32)[:, None, None] * chunk
        + jnp.arange(chunk, dtype=jnp.int32)[None, None, :]
    )
    upper_limit = jnp.stack([root_len, mid_len])[None, :, None]
    upper_ok = (upper_pos < upper_limit).reshape(-1)
    upper_part = partial_attention(
        queries,
        recv_keys.reshape(-1, col_count),
        recv_values.reshape(-1, col_count),
        upper_ok[None, :],
        head_count,
    )
    merged = combine(local_part, upper_part)
    attended = jnp.concatenate([part[2] / part[1] for part in merged], axis=1)
    attention = jnp.where(is_live[:, None], attended, 0.0).astype(jnp.bfloat16)
    return project_over_grp(attention, w_blocks, residual).astype(jnp.bfloat16)


def solution(mesh):
    in_specs = (
        P("tok", "grp"),
        P("tok", "grp"),
        P("tok", "grp"),
        P("tok", "grp"),
        P("grp", None),
        P("tok", None, "grp"),
        P("tok", None, "grp"),
        P(None, "tok", "grp"),
        P(None, "tok", "grp"),
        P(),
        P(),
        P(),
        P(),
        P(),
    )
    out_specs = P("tok", "grp")
    return jax.shard_map(shards, mesh=mesh, in_specs=in_specs, out_specs=out_specs, check_vma=False)
```

```python
import jax
import jax.numpy as jnp
from jax import lax
from jax.sharding import PartitionSpec as P

HEAD_DIM = 128


NEG_FILL = -1e30


def partial_attention(query_rows, key_rows, values, allowed, head_count):
    head_width = query_rows.shape[1] // head_count
    parts = []
    for head in range(head_count):
        cols = slice(head * head_width, (head + 1) * head_width)
        scores = lax.dot_general(
            query_rows[:, cols],
            key_rows[:, cols],
            (((1,), (1,)), ((), ())),
            preferred_element_type=jnp.float32,
        ) * head_width ** (-0.5)
        scores = jnp.where(allowed, scores, NEG_FILL)
        row_max = jnp.max(scores, axis=1, keepdims=True)
        exp_scores = jnp.where(allowed, jnp.exp(scores - row_max), 0.0)
        row_total = jnp.sum(exp_scores, axis=1, keepdims=True)
        weighted = jnp.dot(
            exp_scores.astype(jnp.bfloat16),
            values[:, cols],
            preferred_element_type=jnp.float32,
        )
        parts.append((row_max, row_total, weighted))
    return parts


def combine(earlier, latter):
    merged = []
    for (max_a, total_a, sum_a), (max_b, total_b, sum_b) in zip(earlier, latter):
        new_max = jnp.maximum(max_a, max_b)
        scale_a = jnp.exp(max_a - new_max)
        scale_b = jnp.exp(max_b - new_max)
        merged.append(
            (new_max, total_a * scale_a + total_b * scale_b, sum_a * scale_a + sum_b * scale_b)
        )
    return merged


def project_over_grp(attention, w_blocks, residual):
    size = lax.axis_size("grp")
    index = lax.axis_index("grp")
    block = w_blocks[0].shape[1]
    kept = [jnp.dot(attention, w, preferred_element_type=jnp.float32) for w in w_blocks]
    step = 1
    while step < size:
        high = (index & step) != 0
        keep = [jnp.where(high, kept[k + 1], kept[k]) for k in range(0, len(kept), 2)]
        give = jnp.concatenate(
            [jnp.where(high, kept[k], kept[k + 1]) for k in range(0, len(kept), 2)], axis=1
        )
        give = give.astype(jnp.bfloat16)
        moved = lax.ppermute(give, "grp", [(g, g ^ step) for g in range(size)]).astype(jnp.float32)
        if step * 2 == size:
            keep = [part + residual.astype(jnp.float32) for part in keep]
        kept = [part + moved[:, k * block : (k + 1) * block] for k, part in enumerate(keep)]
        step *= 2
    return kept[0]


def pick(table, index):
    ids = jnp.arange(table.shape[0], dtype=jnp.int32)
    return jnp.sum(jnp.where(ids == index, table, 0))


def shards(
    queries,
    new_keys,
    new_values,
    residual,
    w_out,
    leaf_keys,
    leaf_values,
    upper_keys,
    upper_values,
    req_len,
    leaf_mid,
    mid_root,
    upper_len,
    leaf_len,
):
    dev_count = lax.axis_size("tok")
    my_index = lax.axis_index("tok")
    row_count = queries.shape[0]
    col_count = queries.shape[1]
    head_count = col_count // HEAD_DIM
    mid_count = mid_root.shape[0]
    node_count = upper_len.shape[0]
    root_count = node_count - mid_count
    chunk = upper_keys.shape[1]

    dest_mid = leaf_mid.astype(jnp.int32)
    mid_ids = jnp.arange(mid_count, dtype=jnp.int32)
    dest_root = jnp.sum(
        jnp.where(dest_mid[:, None] == mid_ids[None, :], mid_root[None, :], 0), axis=1
    )
    dest_nodes = jnp.stack([dest_root, root_count + dest_mid], axis=1)
    both = jnp.concatenate([upper_keys, upper_values], axis=0)
    send = both.at[jnp.concatenate([dest_nodes, node_count + dest_nodes], axis=1)].get(
        mode="promise_in_bounds"
    )
    received = lax.all_to_all(send, "tok", 0, 0, tiled=True)
    recv_keys = received[:, :2]
    recv_values = received[:, 2:]

    my_length = pick(req_len, my_index)
    my_mid = pick(leaf_mid, my_index)
    my_leaf_len = pick(leaf_len, my_index)
    my_root = pick(mid_root, my_mid)
    root_len = pick(upper_len, my_root)
    mid_len = pick(upper_len, root_count + my_mid)
    position = jnp.arange(row_count, dtype=jnp.int32)
    is_live = position < my_length
    leaf_count = leaf_keys.shape[1]
    local_keys = jnp.concatenate([leaf_keys[0], new_keys], axis=0)
    local_values = jnp.concatenate([leaf_values[0], new_values], axis=0)
    leaf_allowed = jnp.broadcast_to(
        (jnp.arange(leaf_count) < my_leaf_len)[None, :], (row_count, leaf_count)
    )
    new_allowed = (position[None, :] <= position[:, None]) & is_live[None, :]
    local_part = partial_attention(
        queries,
        local_keys,
        local_values,
        jnp.concatenate([leaf_allowed, new_allowed], axis=1),
        head_count,
    )
    grp_size = lax.axis_size("grp")
    block = w_out.shape[1] // grp_size
    w_blocks = [w_out[:, b * block : (b + 1) * block] for b in range(grp_size)]
    w_blocks, local_part = lax.optimization_barrier((w_blocks, local_part))

    upper_pos = (
        jnp.arange(dev_count, dtype=jnp.int32)[:, None, None] * chunk
        + jnp.arange(chunk, dtype=jnp.int32)[None, None, :]
    )
    upper_limit = jnp.stack([root_len, mid_len])[None, :, None]
    upper_ok = (upper_pos < upper_limit).reshape(-1)
    half = row_count // 2 if row_count % 16 == 0 else row_count
    outputs = []
    for start in range(0, row_count, half):
        rows = slice(start, start + half)
        upper_part = partial_attention(
            queries[rows],
            recv_keys.reshape(-1, col_count),
            recv_values.reshape(-1, col_count),
            upper_ok[None, :],
            head_count,
        )
        merged = combine([tuple(x[rows] for x in part) for part in local_part], upper_part)
        attended = jnp.concatenate([part[2] / part[1] for part in merged], axis=1)
        attention = jnp.where(is_live[rows, None], attended, 0.0).astype(jnp.bfloat16)
        outputs.append(project_over_grp(attention, w_blocks, residual[rows]).astype(jnp.bfloat16))
    return jnp.concatenate(outputs, axis=0)


def solution(mesh):
    in_specs = (
        P("tok", "grp"),
        P("tok", "grp"),
        P("tok", "grp"),
        P("tok", "grp"),
        P("grp", None),
        P("tok", None, "grp"),
        P("tok", None, "grp"),
        P(None, "tok", "grp"),
        P(None, "tok", "grp"),
        P(),
        P(),
        P(),
        P(),
        P(),
    )
    out_specs = P("tok", "grp")
    return jax.shard_map(shards, mesh=mesh, in_specs=in_specs, out_specs=out_specs, check_vma=False)
```

```python
import jax
import jax.numpy as jnp
from jax import lax
from jax.sharding import PartitionSpec as P

HEAD_DIM = 128


NEG_FILL = -1e30


def partial_attention(query_rows, key_rows, values, allowed, head_count):
    head_width = query_rows.shape[1] // head_count
    parts = []
    for head in range(head_count):
        cols = slice(head * head_width, (head + 1) * head_width)
        scores = lax.dot_general(
            query_rows[:, cols],
            key_rows[:, cols],
            (((1,), (1,)), ((), ())),
            preferred_element_type=jnp.float32,
        ) * head_width ** (-0.5)
        scores = jnp.where(allowed, scores, NEG_FILL)
        row_max = jnp.max(scores, axis=1, keepdims=True)
        exp_scores = jnp.where(allowed, jnp.exp(scores - row_max), 0.0)
        row_total = jnp.sum(exp_scores, axis=1, keepdims=True)
        weighted = jnp.dot(
            exp_scores.astype(jnp.bfloat16),
            values[:, cols],
            preferred_element_type=jnp.float32,
        )
        parts.append((row_max, row_total, weighted))
    return parts


def blocked_attention(query_rows, key_rows, values, allowed, head_count):
    rows, cols = query_rows.shape
    head_width = cols // head_count
    head_of_col = jnp.arange(cols, dtype=jnp.int32) // head_width
    spread = jnp.where(
        jnp.arange(head_count, dtype=jnp.int32)[:, None, None] == head_of_col[None, None, :],
        query_rows[None],
        jnp.zeros((), query_rows.dtype),
    ).reshape(head_count * rows, cols)
    scores = lax.dot_general(
        spread, key_rows, (((1,), (1,)), ((), ())), preferred_element_type=jnp.float32
    ) * head_width ** (-0.5)
    scores = jnp.where(allowed, scores, NEG_FILL)
    row_max = jnp.max(scores, axis=1, keepdims=True)
    exp_scores = jnp.where(allowed, jnp.exp(scores - row_max), 0.0)
    row_total = jnp.sum(exp_scores, axis=1, keepdims=True)
    weighted = jnp.dot(exp_scores.astype(jnp.bfloat16), values, preferred_element_type=jnp.float32)
    parts = []
    for head in range(head_count):
        block = slice(head * rows, (head + 1) * rows)
        parts.append((
            row_max[block],
            row_total[block],
            weighted[block, head * head_width : (head + 1) * head_width],
        ))
    return parts


def combine(earlier, latter):
    merged = []
    for (max_a, total_a, sum_a), (max_b, total_b, sum_b) in zip(earlier, latter):
        new_max = jnp.maximum(max_a, max_b)
        scale_a = jnp.exp(max_a - new_max)
        scale_b = jnp.exp(max_b - new_max)
        merged.append(
            (new_max, total_a * scale_a + total_b * scale_b, sum_a * scale_a + sum_b * scale_b)
        )
    return merged


def project_over_grp(attention, w_blocks, residual):
    size = lax.axis_size("grp")
    index = lax.axis_index("grp")
    block = w_blocks[0].shape[1]
    kept = [jnp.dot(attention, w, preferred_element_type=jnp.float32) for w in w_blocks]
    step = 1
    while step < size:
        high = (index & step) != 0
        keep = [jnp.where(high, kept[k + 1], kept[k]) for k in range(0, len(kept), 2)]
        give = jnp.concatenate(
            [jnp.where(high, kept[k], kept[k + 1]) for k in range(0, len(kept), 2)], axis=1
        )
        give = give.astype(jnp.bfloat16)
        moved = lax.ppermute(give, "grp", [(g, g ^ step) for g in range(size)]).astype(jnp.float32)
        if step * 2 == size:
            keep = [part + residual.astype(jnp.float32) for part in keep]
        kept = [part + moved[:, k * block : (k + 1) * block] for k, part in enumerate(keep)]
        step *= 2
    return kept[0]


def pick(table, index):
    ids = jnp.arange(table.shape[0], dtype=jnp.int32)
    return jnp.sum(jnp.where(ids == index, table, 0))


def shards(
    queries,
    new_keys,
    new_values,
    residual,
    w_out,
    leaf_keys,
    leaf_values,
    upper_keys,
    upper_values,
    req_len,
    leaf_mid,
    mid_root,
    upper_len,
    leaf_len,
):
    dev_count = lax.axis_size("tok")
    my_index = lax.axis_index("tok")
    row_count = queries.shape[0]
    col_count = queries.shape[1]
    head_count = col_count // HEAD_DIM
    mid_count = mid_root.shape[0]
    node_count = upper_len.shape[0]
    root_count = node_count - mid_count
    chunk = upper_keys.shape[1]

    dest_mid = leaf_mid.astype(jnp.int32)
    mid_ids = jnp.arange(mid_count, dtype=jnp.int32)
    dest_root = jnp.sum(
        jnp.where(dest_mid[:, None] == mid_ids[None, :], mid_root[None, :], 0), axis=1
    )
    dest_nodes = jnp.stack([dest_root, root_count + dest_mid], axis=1)
    both = jnp.concatenate([upper_keys, upper_values], axis=0)
    send = both.at[jnp.concatenate([dest_nodes, node_count + dest_nodes], axis=1)].get(
        mode="promise_in_bounds"
    )
    received = lax.all_to_all(send, "tok", 0, 0, tiled=True)
    recv_keys = received[:, :2]
    recv_values = received[:, 2:]

    my_length = pick(req_len, my_index)
    my_mid = pick(leaf_mid, my_index)
    my_leaf_len = pick(leaf_len, my_index)
    my_root = pick(mid_root, my_mid)
    root_len = pick(upper_len, my_root)
    mid_len = pick(upper_len, root_count + my_mid)
    position = jnp.arange(row_count, dtype=jnp.int32)
    is_live = position < my_length
    leaf_count = leaf_keys.shape[1]
    local_keys = jnp.concatenate([leaf_keys[0], new_keys], axis=0)
    local_values = jnp.concatenate([leaf_values[0], new_values], axis=0)
    leaf_allowed = jnp.broadcast_to(
        (jnp.arange(leaf_count) < my_leaf_len)[None, :], (row_count, leaf_count)
    )
    new_allowed = (position[None, :] <= position[:, None]) & is_live[None, :]
    local_part = partial_attention(
        queries,
        local_keys,
        local_values,
        jnp.concatenate([leaf_allowed, new_allowed], axis=1),
        head_count,
    )
    grp_size = lax.axis_size("grp")
    block = w_out.shape[1] // grp_size
    w_blocks = [w_out[:, b * block : (b + 1) * block] for b in range(grp_size)]
    w_blocks, local_part = lax.optimization_barrier((w_blocks, local_part))

    upper_pos = (
        jnp.arange(dev_count, dtype=jnp.int32)[:, None, None] * chunk
        + jnp.arange(chunk, dtype=jnp.int32)[None, None, :]
    )
    upper_limit = jnp.stack([root_len, mid_len])[None, :, None]
    upper_ok = (upper_pos < upper_limit).reshape(-1)
    upper_part = blocked_attention(
        queries,
        recv_keys.reshape(-1, col_count),
        recv_values.reshape(-1, col_count),
        upper_ok[None, :],
        head_count,
    )
    merged = combine(local_part, upper_part)
    attended = jnp.concatenate([part[2] / part[1] for part in merged], axis=1)
    attention = jnp.where(is_live[:, None], attended, 0.0).astype(jnp.bfloat16)
    return project_over_grp(attention, w_blocks, residual).astype(jnp.bfloat16)


def solution(mesh):
    in_specs = (
        P("tok", "grp"),
        P("tok", "grp"),
        P("tok", "grp"),
        P("tok", "grp"),
        P("grp", None),
        P("tok", None, "grp"),
        P("tok", None, "grp"),
        P(None, "tok", "grp"),
        P(None, "tok", "grp"),
        P(),
        P(),
        P(),
        P(),
        P(),
    )
    out_specs = P("tok", "grp")
    return jax.shard_map(shards, mesh=mesh, in_specs=in_specs, out_specs=out_specs, check_vma=False)
```

```python
import jax
import jax.numpy as jnp
from jax import lax
from jax.sharding import PartitionSpec as P

HEAD_DIM = 128


NEG_FILL = -1e30


def partial_attention(query_rows, key_rows, values, allowed, head_count):
    head_width = query_rows.shape[1] // head_count
    parts = []
    for head in range(head_count):
        cols = slice(head * head_width, (head + 1) * head_width)
        scores = lax.dot_general(
            query_rows[:, cols],
            key_rows[:, cols],
            (((1,), (1,)), ((), ())),
            preferred_element_type=jnp.float32,
        ) * head_width ** (-0.5)
        scores = jnp.where(allowed, scores, NEG_FILL)
        row_max = jnp.max(scores, axis=1, keepdims=True)
        exp_scores = jnp.where(allowed, jnp.exp(scores - row_max), 0.0)
        row_total = jnp.sum(exp_scores, axis=1, keepdims=True)
        weighted = jnp.dot(
            exp_scores.astype(jnp.bfloat16),
            values[:, cols],
            preferred_element_type=jnp.float32,
        )
        parts.append((row_max, row_total, weighted))
    return parts


def combine(earlier, latter):
    merged = []
    for (max_a, total_a, sum_a), (max_b, total_b, sum_b) in zip(earlier, latter):
        new_max = jnp.maximum(max_a, max_b)
        scale_a = jnp.exp(max_a - new_max)
        scale_b = jnp.exp(max_b - new_max)
        merged.append(
            (new_max, total_a * scale_a + total_b * scale_b, sum_a * scale_a + sum_b * scale_b)
        )
    return merged


def project_over_grp(attention, w_blocks, residual):
    size = lax.axis_size("grp")
    index = lax.axis_index("grp")
    block = w_blocks[0].shape[1]
    kept = [jnp.dot(attention, w, preferred_element_type=jnp.float32) for w in w_blocks]
    step = 1
    while step < size:
        high = (index & step) != 0
        keep = [jnp.where(high, kept[k + 1], kept[k]) for k in range(0, len(kept), 2)]
        give = jnp.concatenate(
            [jnp.where(high, kept[k], kept[k + 1]) for k in range(0, len(kept), 2)], axis=1
        )
        give = give.astype(jnp.bfloat16)
        moved = lax.ppermute(give, "grp", [(g, g ^ step) for g in range(size)]).astype(jnp.float32)
        if step * 2 == size:
            keep = [part + residual.astype(jnp.float32) for part in keep]
        kept = [part + moved[:, k * block : (k + 1) * block] for k, part in enumerate(keep)]
        step *= 2
    return kept[0]


def pick(table, index):
    ids = jnp.arange(table.shape[0], dtype=jnp.int32)
    return jnp.sum(jnp.where(ids == index, table, 0))


def shards(
    queries,
    new_keys,
    new_values,
    residual,
    w_out,
    leaf_keys,
    leaf_values,
    upper_keys,
    upper_values,
    req_len,
    leaf_mid,
    mid_root,
    upper_len,
    leaf_len,
):
    dev_count = lax.axis_size("tok")
    my_index = lax.axis_index("tok")
    row_count = queries.shape[0]
    col_count = queries.shape[1]
    head_count = col_count // HEAD_DIM
    mid_count = mid_root.shape[0]
    node_count = upper_len.shape[0]
    root_count = node_count - mid_count
    chunk = upper_keys.shape[1]

    dest_mid = leaf_mid.astype(jnp.int32)
    mid_ids = jnp.arange(mid_count, dtype=jnp.int32)
    dest_root = jnp.sum(
        jnp.where(dest_mid[:, None] == mid_ids[None, :], mid_root[None, :], 0), axis=1
    )
    dest_nodes = jnp.stack([dest_root, root_count + dest_mid], axis=1)
    recv_keys = lax.all_to_all(
        upper_keys.at[dest_nodes].get(mode="promise_in_bounds"), "tok", 0, 0, tiled=True
    )
    recv_values = lax.all_to_all(
        upper_values.at[dest_nodes].get(mode="promise_in_bounds"), "tok", 0, 0, tiled=True
    )

    my_length = pick(req_len, my_index)
    my_mid = pick(leaf_mid, my_index)
    my_leaf_len = pick(leaf_len, my_index)
    my_root = pick(mid_root, my_mid)
    root_len = pick(upper_len, my_root)
    mid_len = pick(upper_len, root_count + my_mid)
    position = jnp.arange(row_count, dtype=jnp.int32)
    is_live = position < my_length
    leaf_count = leaf_keys.shape[1]
    local_keys = jnp.concatenate([leaf_keys[0], new_keys], axis=0)
    local_values = jnp.concatenate([leaf_values[0], new_values], axis=0)
    leaf_allowed = jnp.broadcast_to(
        (jnp.arange(leaf_count) < my_leaf_len)[None, :], (row_count, leaf_count)
    )
    new_allowed = (position[None, :] <= position[:, None]) & is_live[None, :]
    local_part = partial_attention(
        queries,
        local_keys,
        local_values,
        jnp.concatenate([leaf_allowed, new_allowed], axis=1),
        head_count,
    )
    grp_size = lax.axis_size("grp")
    block = w_out.shape[1] // grp_size
    w_blocks = [w_out[:, b * block : (b + 1) * block] for b in range(grp_size)]
    w_blocks, local_part = lax.optimization_barrier((w_blocks, local_part))

    upper_pos = (
        jnp.arange(dev_count, dtype=jnp.int32)[:, None, None] * chunk
        + jnp.arange(chunk, dtype=jnp.int32)[None, None, :]
    )
    upper_limit = jnp.stack([root_len, mid_len])[None, :, None]
    upper_ok = (upper_pos < upper_limit).reshape(-1)
    upper_part = partial_attention(
        queries,
        recv_keys.reshape(-1, col_count),
        recv_values.reshape(-1, col_count),
        upper_ok[None, :],
        head_count,
    )
    merged = combine(local_part, upper_part)
    attended = jnp.concatenate([part[2] / part[1] for part in merged], axis=1)
    attention = jnp.where(is_live[:, None], attended, 0.0).astype(jnp.bfloat16)
    return project_over_grp(attention, w_blocks, residual).astype(jnp.bfloat16)


def solution(mesh):
    in_specs = (
        P("tok", "grp"),
        P("tok", "grp"),
        P("tok", "grp"),
        P("tok", "grp"),
        P("grp", None),
        P("tok", None, "grp"),
        P("tok", None, "grp"),
        P(None, "tok", "grp"),
        P(None, "tok", "grp"),
        P(),
        P(),
        P(),
        P(),
        P(),
    )
    out_specs = P("tok", "grp")
    return jax.shard_map(shards, mesh=mesh, in_specs=in_specs, out_specs=out_specs, check_vma=False)
```

```python
import jax
import jax.numpy as jnp
from jax import lax
from jax.sharding import PartitionSpec as P

HEAD_DIM = 128


NEG_FILL = -1e30


def partial_attention(query_rows, key_rows, values, allowed, head_count, some_allowed=False):
    head_width = query_rows.shape[1] // head_count
    parts = []
    for head in range(head_count):
        cols = slice(head * head_width, (head + 1) * head_width)
        scores = lax.dot_general(
            query_rows[:, cols],
            key_rows[:, cols],
            (((1,), (1,)), ((), ())),
            preferred_element_type=jnp.float32,
        ) * head_width ** (-0.5)
        scores = jnp.where(allowed, scores, NEG_FILL)
        row_max = jnp.max(scores, axis=1, keepdims=True)
        exp_scores = jnp.exp(scores - row_max)
        if not some_allowed:
            exp_scores = jnp.where(allowed, exp_scores, 0.0)
        row_total = jnp.sum(exp_scores, axis=1, keepdims=True)
        weighted = jnp.dot(
            exp_scores.astype(jnp.bfloat16),
            values[:, cols],
            preferred_element_type=jnp.float32,
        )
        parts.append((row_max, row_total, weighted))
    return parts


def combine(earlier, latter):
    merged = []
    for (max_a, total_a, sum_a), (max_b, total_b, sum_b) in zip(earlier, latter):
        new_max = jnp.maximum(max_a, max_b)
        scale_a = jnp.exp(max_a - new_max)
        scale_b = jnp.exp(max_b - new_max)
        merged.append(
            (new_max, total_a * scale_a + total_b * scale_b, sum_a * scale_a + sum_b * scale_b)
        )
    return merged


def project_over_grp(attention, w_blocks, residual):
    size = lax.axis_size("grp")
    index = lax.axis_index("grp")
    block = w_blocks[0].shape[1]
    kept = [jnp.dot(attention, w, preferred_element_type=jnp.float32) for w in w_blocks]
    step = 1
    while step < size:
        high = (index & step) != 0
        keep = [jnp.where(high, kept[k + 1], kept[k]) for k in range(0, len(kept), 2)]
        give = jnp.concatenate(
            [jnp.where(high, kept[k], kept[k + 1]) for k in range(0, len(kept), 2)], axis=1
        )
        give = give.astype(jnp.bfloat16)
        moved = lax.ppermute(give, "grp", [(g, g ^ step) for g in range(size)]).astype(jnp.float32)
        if step * 2 == size:
            keep = [part + residual.astype(jnp.float32) for part in keep]
        kept = [part + moved[:, k * block : (k + 1) * block] for k, part in enumerate(keep)]
        step *= 2
    return kept[0]


def pick(table, index):
    ids = jnp.arange(table.shape[0], dtype=jnp.int32)
    return jnp.sum(jnp.where(ids == index, table, 0))


def shards(
    queries,
    new_keys,
    new_values,
    residual,
    w_out,
    leaf_keys,
    leaf_values,
    upper_keys,
    upper_values,
    req_len,
    leaf_mid,
    mid_root,
    upper_len,
    leaf_len,
):
    dev_count = lax.axis_size("tok")
    my_index = lax.axis_index("tok")
    row_count = queries.shape[0]
    col_count = queries.shape[1]
    head_count = col_count // HEAD_DIM
    mid_count = mid_root.shape[0]
    node_count = upper_len.shape[0]
    root_count = node_count - mid_count
    chunk = upper_keys.shape[1]

    dest_mid = leaf_mid.astype(jnp.int32)
    mid_ids = jnp.arange(mid_count, dtype=jnp.int32)
    dest_root = jnp.sum(
        jnp.where(dest_mid[:, None] == mid_ids[None, :], mid_root[None, :], 0), axis=1
    )
    dest_nodes = jnp.stack([dest_root, root_count + dest_mid], axis=1)
    both = jnp.concatenate([upper_keys, upper_values], axis=0)
    send = both.at[jnp.concatenate([dest_nodes, node_count + dest_nodes], axis=1)].get(
        mode="promise_in_bounds"
    )
    received = lax.all_to_all(send, "tok", 0, 0, tiled=True)
    recv_keys = received[:, :2]
    recv_values = received[:, 2:]

    my_length = pick(req_len, my_index)
    my_mid = pick(leaf_mid, my_index)
    my_leaf_len = pick(leaf_len, my_index)
    my_root = pick(mid_root, my_mid)
    root_len = pick(upper_len, my_root)
    mid_len = pick(upper_len, root_count + my_mid)
    position = jnp.arange(row_count, dtype=jnp.int32)
    is_live = position < my_length
    leaf_count = leaf_keys.shape[1]
    local_keys = jnp.concatenate([leaf_keys[0], new_keys], axis=0)
    local_values = jnp.concatenate([leaf_values[0], new_values], axis=0)
    leaf_allowed = jnp.broadcast_to(
        (jnp.arange(leaf_count) < my_leaf_len)[None, :], (row_count, leaf_count)
    )
    new_allowed = (position[None, :] <= position[:, None]) & is_live[None, :]
    local_part = partial_attention(
        queries,
        local_keys,
        local_values,
        jnp.concatenate([leaf_allowed, new_allowed], axis=1),
        head_count,
    )
    grp_size = lax.axis_size("grp")
    block = w_out.shape[1] // grp_size
    w_blocks = [w_out[:, b * block : (b + 1) * block] for b in range(grp_size)]
    w_blocks, local_part = lax.optimization_barrier((w_blocks, local_part))

    upper_pos = (
        jnp.arange(dev_count, dtype=jnp.int32)[:, None, None] * chunk
        + jnp.arange(chunk, dtype=jnp.int32)[None, None, :]
    )
    upper_limit = jnp.stack([root_len, mid_len])[None, :, None]
    upper_ok = (upper_pos < upper_limit).reshape(-1)
    upper_part = partial_attention(
        queries,
        recv_keys.reshape(-1, col_count),
        recv_values.reshape(-1, col_count),
        upper_ok[None, :],
        head_count,
        some_allowed=True,
    )
    merged = combine(local_part, upper_part)
    attended = jnp.concatenate([part[2] / part[1] for part in merged], axis=1)
    attention = jnp.where(is_live[:, None], attended, 0.0).astype(jnp.bfloat16)
    return project_over_grp(attention, w_blocks, residual).astype(jnp.bfloat16)


def solution(mesh):
    in_specs = (
        P("tok", "grp"),
        P("tok", "grp"),
        P("tok", "grp"),
        P("tok", "grp"),
        P("grp", None),
        P("tok", None, "grp"),
        P("tok", None, "grp"),
        P(None, "tok", "grp"),
        P(None, "tok", "grp"),
        P(),
        P(),
        P(),
        P(),
        P(),
    )
    out_specs = P("tok", "grp")
    return jax.shard_map(shards, mesh=mesh, in_specs=in_specs, out_specs=out_specs, check_vma=False)
```

```python
import jax
import jax.numpy as jnp
from jax import lax
from jax.sharding import PartitionSpec as P

HEAD_DIM = 128


NEG_FILL = -1e30


def partial_attention(query_rows, key_rows, values, allowed, head_count):
    head_width = query_rows.shape[1] // head_count
    parts = []
    for head in range(head_count):
        cols = slice(head * head_width, (head + 1) * head_width)
        scores = lax.dot_general(
            query_rows[:, cols],
            key_rows[:, cols],
            (((1,), (1,)), ((), ())),
            preferred_element_type=jnp.float32,
        ) * head_width ** (-0.5)
        scores = jnp.where(allowed, scores, NEG_FILL)
        row_max = jnp.max(scores, axis=1, keepdims=True)
        exp_scores = jnp.where(allowed, jnp.exp(scores - row_max), 0.0)
        row_total = jnp.sum(exp_scores, axis=1, keepdims=True)
        weighted = jnp.dot(
            exp_scores.astype(jnp.bfloat16),
            values[:, cols],
            preferred_element_type=jnp.float32,
        )
        parts.append((row_max, row_total, weighted))
    return parts


def combine(earlier, latter):
    merged = []
    for (max_a, total_a, sum_a), (max_b, total_b, sum_b) in zip(earlier, latter):
        new_max = jnp.maximum(max_a, max_b)
        scale_a = jnp.exp(max_a - new_max)
        scale_b = jnp.exp(max_b - new_max)
        merged.append(
            (new_max, total_a * scale_a + total_b * scale_b, sum_a * scale_a + sum_b * scale_b)
        )
    return merged


def project_over_grp(attention, w_blocks, residual):
    size = lax.axis_size("grp")
    index = lax.axis_index("grp")
    block = w_blocks[0].shape[1]
    projected = jnp.dot(
        attention, jnp.concatenate(w_blocks, axis=1), preferred_element_type=jnp.float32
    )
    kept = [projected[:, b * block : (b + 1) * block] for b in range(size)]
    step = 1
    while step < size:
        high = (index & step) != 0
        keep = [jnp.where(high, kept[k + 1], kept[k]) for k in range(0, len(kept), 2)]
        give = jnp.concatenate(
            [jnp.where(high, kept[k], kept[k + 1]) for k in range(0, len(kept), 2)], axis=1
        )
        give = give.astype(jnp.bfloat16)
        moved = lax.ppermute(give, "grp", [(g, g ^ step) for g in range(size)]).astype(jnp.float32)
        if step * 2 == size:
            keep = [part + residual.astype(jnp.float32) for part in keep]
        kept = [part + moved[:, k * block : (k + 1) * block] for k, part in enumerate(keep)]
        step *= 2
    return kept[0]


def pick(table, index):
    ids = jnp.arange(table.shape[0], dtype=jnp.int32)
    return jnp.sum(jnp.where(ids == index, table, 0))


def shards(
    queries,
    new_keys,
    new_values,
    residual,
    w_out,
    leaf_keys,
    leaf_values,
    upper_keys,
    upper_values,
    req_len,
    leaf_mid,
    mid_root,
    upper_len,
    leaf_len,
):
    dev_count = lax.axis_size("tok")
    my_index = lax.axis_index("tok")
    row_count = queries.shape[0]
    col_count = queries.shape[1]
    head_count = col_count // HEAD_DIM
    mid_count = mid_root.shape[0]
    node_count = upper_len.shape[0]
    root_count = node_count - mid_count
    chunk = upper_keys.shape[1]

    dest_mid = leaf_mid.astype(jnp.int32)
    mid_ids = jnp.arange(mid_count, dtype=jnp.int32)
    dest_root = jnp.sum(
        jnp.where(dest_mid[:, None] == mid_ids[None, :], mid_root[None, :], 0), axis=1
    )
    dest_nodes = jnp.stack([dest_root, root_count + dest_mid], axis=1)
    both = jnp.concatenate([upper_keys, upper_values], axis=0)
    send = both.at[jnp.concatenate([dest_nodes, node_count + dest_nodes], axis=1)].get(
        mode="promise_in_bounds"
    )
    received = lax.all_to_all(send, "tok", 0, 0, tiled=True)
    recv_keys = received[:, :2]
    recv_values = received[:, 2:]

    my_length = pick(req_len, my_index)
    my_mid = pick(leaf_mid, my_index)
    my_leaf_len = pick(leaf_len, my_index)
    my_root = pick(mid_root, my_mid)
    root_len = pick(upper_len, my_root)
    mid_len = pick(upper_len, root_count + my_mid)
    position = jnp.arange(row_count, dtype=jnp.int32)
    is_live = position < my_length
    leaf_count = leaf_keys.shape[1]
    local_keys = jnp.concatenate([leaf_keys[0], new_keys], axis=0)
    local_values = jnp.concatenate([leaf_values[0], new_values], axis=0)
    leaf_allowed = jnp.broadcast_to(
        (jnp.arange(leaf_count) < my_leaf_len)[None, :], (row_count, leaf_count)
    )
    new_allowed = (position[None, :] <= position[:, None]) & is_live[None, :]
    local_part = partial_attention(
        queries,
        local_keys,
        local_values,
        jnp.concatenate([leaf_allowed, new_allowed], axis=1),
        head_count,
    )
    grp_size = lax.axis_size("grp")
    block = w_out.shape[1] // grp_size
    w_blocks = [w_out[:, b * block : (b + 1) * block] for b in range(grp_size)]
    w_blocks, local_part = lax.optimization_barrier((w_blocks, local_part))

    upper_pos = (
        jnp.arange(dev_count, dtype=jnp.int32)[:, None, None] * chunk
        + jnp.arange(chunk, dtype=jnp.int32)[None, None, :]
    )
    upper_limit = jnp.stack([root_len, mid_len])[None, :, None]
    upper_ok = (upper_pos < upper_limit).reshape(-1)
    upper_part = partial_attention(
        queries,
        recv_keys.reshape(-1, col_count),
        recv_values.reshape(-1, col_count),
        upper_ok[None, :],
        head_count,
    )
    merged = combine(local_part, upper_part)
    attended = jnp.concatenate([part[2] / part[1] for part in merged], axis=1)
    attention = jnp.where(is_live[:, None], attended, 0.0).astype(jnp.bfloat16)
    return project_over_grp(attention, w_blocks, residual).astype(jnp.bfloat16)


def solution(mesh):
    in_specs = (
        P("tok", "grp"),
        P("tok", "grp"),
        P("tok", "grp"),
        P("tok", "grp"),
        P("grp", None),
        P("tok", None, "grp"),
        P("tok", None, "grp"),
        P(None, "tok", "grp"),
        P(None, "tok", "grp"),
        P(),
        P(),
        P(),
        P(),
        P(),
    )
    out_specs = P("tok", "grp")
    return jax.shard_map(shards, mesh=mesh, in_specs=in_specs, out_specs=out_specs, check_vma=False)
```
